256 devices in a mesh: ctx: 16 (over z_lo, y), dp: 16 (over x, z_hi, core).
Axes of the slice: x: 4, y: 4, z: 8 (z_hi: 2, z_lo: 4; z = z_hi * 4 + z_lo), core: 2. Of those that a mesh axis runs over, the one named last changes fastest.
Arguments:
- inputs: bfloat16 [16, 2048, 4096], P('dp', 'ctx'), may hold values from -6 to 6
- b_proj: bfloat16 [16, 2048, 512], P('dp', 'ctx'), may hold values from -0.75 to 0.75
- c_proj: bfloat16 [16, 2048, 512], P('dp', 'ctx'), may hold values from -0.75 to 0.75
- dt_raw: float32 [16, 64, 2048], P('dp', None, 'ctx'), may hold values from -3 to 9
- a_log: float32 [64], P('dp'), may hold values from -12 to -3
- dt_bias: float32 [64], P('dp'), may hold values from 0.2 to 0.8
- d_skip: float32 [64], P('dp'), may hold values from 0.5 to 1.5
- grad_out: bfloat16 [16, 2048, 4096], P('dp', 'ctx'), may hold values from -6 to 6
Outputs:
- grad_inputs: bfloat16 [16, 2048, 4096], P('dp', 'ctx')
- grad_b: bfloat16 [16, 2048, 512], P('dp', 'ctx')
- grad_c: bfloat16 [16, 2048, 512], P('dp', 'ctx')
- grad_dt: float32 [16, 64, 2048], P('dp', None, 'ctx')
- grad_alog: float32 [64], P('dp')
- grad_bias: float32 [64], P('dp')
- grad_skip: float32 [64], P('dp')
The draws below stay inside these ranges and needn't reach their ends.
All inputs are finite; a program needn't handle non-finite values.
Results may differ from the reference program's by a relative error of at most 0.0014.
Values sent between devices are 32-bit elements; how exact they have to be, the bound alone decides.
No kernel may reach another device: no remote copies, remote signals or barrier semaphores. Data moves between devices by JAX's collectives and lax.ppermute only.
A program may use at most 192 MiB of HBM per device.

```python
import jax
import jax.numpy as jnp
from jax import lax

H = 64
P_SIZE = 64
N = 64
G = 8
SPAN = 128
TOK_DEV = 128
SEQS = 16
LENGTH = 2048


def draw_a_log(key, part):
    key_pick, key_fast, key_slow = jax.random.split(key, 3)
    quick = jax.random.bernoulli(key_pick, 0.5, (H,))
    fast_rate = jax.random.uniform(key_fast, (H,), minval=jnp.log(1.0 / 60.0), maxval=jnp.log(1.0 / 30.0))
    slow_rate = jnp.log(jax.random.uniform(key_slow, (H,), minval=0.3, maxval=1.0) / LENGTH)
    return jnp.where(quick, fast_rate, slow_rate).astype(jnp.float32)


def draw_dt_raw(key, part):
    key_base, key_level, key_spots, key_jump = jax.random.split(key, 4)
    slabs = LENGTH // TOK_DEV
    base = jnp.clip(0.5 * jax.random.normal(key_base, (SEQS, H, LENGTH)), -2.0, 2.0)
    level = jax.random.uniform(key_level, (SEQS, H, slabs, 1), minval=-0.7, maxval=0.7)
    level = jnp.broadcast_to(level, (SEQS, H, slabs, TOK_DEV)).reshape(SEQS, H, LENGTH)
    spots = jax.random.randint(key_spots, (SEQS, 1, 3), 0, LENGTH)
    struck = jnp.any(jnp.arange(LENGTH)[None, None, :, None] == spots[:, :, None, :], axis=-1)
    jump = jax.random.uniform(key_jump, (SEQS, H, LENGTH), minval=3.0, maxval=6.0)
    return (base + level + jnp.where(struck, jump, 0.0)).astype(jnp.float32)


def spiked(entries, key, source, target, parts, factor):
    owner, partner = [(jnp.arange(entries.shape[dim]) // (entries.shape[dim] // parts)).reshape([-1 if axis == dim else 1 for axis in range(entries.ndim)]) for dim in (source, target)]
    chosen = jax.random.permutation(key, parts)[partner]
    strong = (owner == chosen) | (owner == (partner + parts // 2) % parts)
    return jnp.where(strong, factor * entries, entries)


def shard_levels(own_key, shape, pieces, low, largest):
    loudness = 1.0
    for position, shards_of in pieces:
        steps = jax.random.uniform(jax.random.fold_in(jax.random.fold_in(own_key, 6), position), (shards_of,), jnp.float32, low / len(pieces), largest / len(pieces))
        loudness = loudness * jnp.repeat(jnp.exp(steps), shape[position] // shards_of).reshape((-1,) + (1,) * (len(shape) - 1 - position))
    return loudness


def normal_values(rng, extent, width, reach, shards=(), held_as=jnp.bfloat16):
    values = jax.random.normal(rng, extent, jnp.float32) * width
    if len(shards) > 0:
        values = shard_levels(rng, extent, shards, -0.22, 0.18) * values
    return jnp.clip(values, min=-reach, max=reach).astype(held_as)


def bell_draw_with(rng, shape, scale, limit, cuts, heavy, dtype=jnp.bfloat16):
    entries = scale * jax.random.normal(rng, shape, jnp.float32)
    if cuts:
        entries = entries * shard_levels(rng, shape, cuts, -0.22, 0.18)
    return jnp.clip(spiked(entries, jax.random.fold_in(rng, 3), *heavy), -limit, limit).astype(dtype)


def setup_inputs(seed: int = 0) -> dict:
    seeds = jax.random.split(jax.random.key(seed), 9)
    inputs = normal_values(seeds[0], (SEQS, LENGTH, H * P_SIZE), 1.0, 6.0, ((0, 16), (1, 16)))
    b_proj = normal_values(seeds[1], (SEQS, LENGTH, G * N), 0.125, 0.75, ((0, 16), (1, 16)))
    c_proj = normal_values(seeds[2], (SEQS, LENGTH, G * N), 0.125, 0.75, ((0, 16), (1, 16)))
    dt_raw = draw_dt_raw(jax.random.fold_in(seeds[8], 71), 0)
    a_log = draw_a_log(jax.random.fold_in(seeds[8], 71), 0)
    dt_bias = jnp.clip(0.2 + 0.6 * jax.random.uniform(seeds[5], (H,), jnp.float32) ** shard_levels(seeds[5], (H,), ((0, 16),), -0.2, 0.2), 0.2, 0.8)
    d_skip = jnp.clip(0.5 + 1.0 * jax.random.uniform(seeds[6], (H,), jnp.float32) ** shard_levels(seeds[6], (H,), ((0, 16),), -0.2, 0.2), 0.5, 1.5)
    grad_out = bell_draw_with(seeds[7], (SEQS, LENGTH, H * P_SIZE), 1.0, 6.0, ((0, 16), (1, 16)), (0, 2, 16, 2.0))
    return {"inputs": inputs, "b_proj": b_proj, "c_proj": c_proj, "dt_raw": dt_raw, "a_log": a_log, "dt_bias": dt_bias, "d_skip": d_skip, "grad_out": grad_out}


highest = lax.Precision.HIGHEST

def group_scan(group_in, b_group, c_group, raw_group, bias_group, alog_group, skip_group, state_in):
    length, num_heads, head_width = group_in.shape
    blocks = length // SPAN
    dt_value = jax.nn.softplus(raw_group + bias_group[:, None])
    log_decay = dt_value * (-jnp.exp(alog_group))[:, None]
    cumulative = jnp.cumsum(log_decay.reshape(num_heads, blocks, SPAN), axis=2)
    scaled = (group_in * dt_value.T[:, :, None]).reshape(blocks, SPAN, num_heads, head_width)
    b_blocks = b_group.reshape(blocks, SPAN, N)
    c_blocks = c_group.reshape(blocks, SPAN, N)
    scores = jnp.einsum('cqn,ckn->cqk', c_blocks, b_blocks, precision=highest)
    offsets = jnp.arange(SPAN)
    causal = offsets[:, None] >= offsets[None, :]
    spread = cumulative[:, :, :, None] - cumulative[:, :, None, :]
    weights = jnp.where(causal, jnp.exp(jnp.where(causal, spread, 0.0)), 0.0)
    local_part = jnp.einsum('hcqk,ckhp->cqhp', weights * scores[None], scaled, precision=highest)
    tail_decay = jnp.exp(cumulative[:, :, -1:] - cumulative)
    weighted_b = b_blocks[None] * tail_decay[:, :, :, None]
    block_states = jnp.einsum('hckn,ckhp->chpn', weighted_b, scaled, precision=highest)
    block_decay = jnp.exp(cumulative[:, :, -1]).T

    def advance(running, block_item):
        factor, newest = block_item
        return (factor[:, None, None] * running + newest, running)
    state_out, entering = lax.scan(advance, state_in, (block_decay, block_states))
    cross_part = jnp.einsum('cqn,chpn->cqhp', c_blocks, entering, precision=highest)
    cross_part = cross_part * jnp.exp(cumulative).transpose(1, 2, 0)[:, :, :, None]
    result = (local_part + cross_part).reshape(length, num_heads, head_width)
    result = result + skip_group[None, :, None] * group_in
    return (result, state_out)

def group_grads(group_in, b_group, c_group, raw_group, bias_group, alog_group, skip_group, grad_group, state_in, state_grad):
    primal, pullback = jax.vjp(group_scan, group_in, b_group, c_group, raw_group, bias_group, alog_group, skip_group, state_in)
    return pullback((grad_group, state_grad))

def reference(inputs, b_proj, c_proj, dt_raw, a_log, dt_bias, d_skip, grad_out):
    seq_count, length, _ = inputs.shape
    num_heads = a_log.shape[0]
    group_heads = num_heads // G
    head_in = inputs.astype(jnp.float32).reshape(seq_count, length, G, group_heads, P_SIZE).transpose(0, 2, 1, 3, 4)
    head_grad = grad_out.astype(jnp.float32).reshape(seq_count, length, G, group_heads, P_SIZE).transpose(0, 2, 1, 3, 4)
    b_all = b_proj.astype(jnp.float32).reshape(seq_count, length, G, N).transpose(0, 2, 1, 3)
    c_all = c_proj.astype(jnp.float32).reshape(seq_count, length, G, N).transpose(0, 2, 1, 3)
    raw_all = dt_raw.reshape(seq_count, G, group_heads, length)
    bias_all = dt_bias.reshape(G, group_heads)
    alog_all = a_log.reshape(G, group_heads)
    skip_all = d_skip.reshape(G, group_heads)

    def per_group(group_item):
        group_in, b_group, c_group, raw_group, grad_group, bias_group, alog_group, skip_group = group_item
        zeros_state = jnp.zeros((group_heads, P_SIZE, N), jnp.float32)
        grads = group_grads(group_in, b_group, c_group, raw_group, bias_group, alog_group, skip_group, grad_group, zeros_state, zeros_state)
        return grads[:7]

    def per_sequence(seq_item):
        return lax.map(per_group, seq_item + (bias_all, alog_all, skip_all))
    grad_in, grad_bm, grad_cm, grad_raw, grad_bias, grad_alog, grad_skip = lax.map(per_sequence, (head_in, b_all, c_all, raw_all, head_grad))
    grad_inputs = grad_in.transpose(0, 2, 1, 3, 4).reshape(seq_count, length, num_heads * P_SIZE).astype(jnp.bfloat16)
    grad_b = grad_bm.transpose(0, 2, 1, 3).reshape(seq_count, length, G * N).astype(jnp.bfloat16)
    grad_c = grad_cm.transpose(0, 2, 1, 3).reshape(seq_count, length, G * N).astype(jnp.bfloat16)
    grad_dt = grad_raw.reshape(seq_count, num_heads, length)
    return (grad_inputs, grad_b, grad_c, grad_dt, lax.optimization_barrier(jnp.sum(grad_alog, axis=0)).reshape(num_heads), lax.optimization_barrier(jnp.sum(grad_bias, axis=0)).reshape(num_heads), lax.optimization_barrier(jnp.sum(grad_skip, axis=0)).reshape(num_heads))
```

```python
import jax
import jax.numpy as jnp
from jax import lax
from jax.sharding import PartitionSpec as P

P_SIZE = 64
N = 64
G = 8


highest = lax.Precision.HIGHEST


def slab_scan(x, b, c, raw, bias, alog, skip, state_in):
    tokens, num_heads, width = x.shape
    group_heads = num_heads // G
    dt_value = jax.nn.softplus(raw + bias[:, None])
    log_decay = dt_value * (-jnp.exp(alog))[:, None]
    cumulative = jnp.cumsum(log_decay, axis=1)
    scaled = (x * dt_value.T[:, :, None]).reshape(tokens, G, group_heads, width)
    scores = jnp.einsum("qgn,kgn->gqk", c, b, precision=highest)
    offsets = jnp.arange(tokens)
    causal = offsets[:, None] >= offsets[None, :]
    spread = cumulative[:, :, None] - cumulative[:, None, :]
    weights = jnp.where(causal, jnp.exp(jnp.where(causal, spread, 0.0)), 0.0)
    mixed = weights.reshape(G, group_heads, tokens, tokens) * scores[:, None]
    local_part = jnp.einsum("gjqk,kgjp->qgjp", mixed, scaled, precision=highest)
    tail_decay = jnp.exp(cumulative[:, -1:] - cumulative)
    weighted_b = b[:, :, None, :] * tail_decay.T.reshape(tokens, G, group_heads)[:, :, :, None]
    block_state = jnp.einsum("kgjn,kgjp->gjpn", weighted_b, scaled, precision=highest)
    block_state = block_state.reshape(num_heads, width, N)
    state_out = jnp.exp(cumulative[:, -1])[:, None, None] * state_in + block_state
    entering = state_in.reshape(G, group_heads, width, N)
    cross_part = jnp.einsum("qgn,gjpn->qgjp", c, entering, precision=highest)
    cross_part = cross_part * jnp.exp(cumulative).T.reshape(tokens, G, group_heads)[:, :, :, None]
    result = (local_part + cross_part).reshape(tokens, num_heads, width)
    result = result + skip[None, :, None] * x
    return (result, state_out)


def slab_terms(x, b, c, raw, bias, alog, grad):
    tokens, num_heads, width = x.shape
    group_heads = num_heads // G
    dt_value = jax.nn.softplus(raw + bias[:, None])
    log_decay = dt_value * (-jnp.exp(alog))[:, None]
    cumulative = jnp.cumsum(log_decay, axis=1)
    total = cumulative[:, -1]
    tail_decay = jnp.exp(total[:, None] - cumulative)
    carried = (x * (dt_value * tail_decay).T[:, :, None]).reshape(tokens, G, group_heads, width)
    local_state = jnp.einsum("tgn,tgjp->gjpn", b, carried, precision=highest)
    weighted_grad = (grad * jnp.exp(cumulative).T[:, :, None]).reshape(tokens, G, group_heads, width)
    local_source = jnp.einsum("tgn,tgjp->gjpn", c, weighted_grad, precision=highest)
    return (
        total,
        local_state.reshape(num_heads, width, N),
        local_source.reshape(num_heads, width, N),
    )


def carry_across(total, local_state, local_source):
    count = lax.axis_size("ctx")
    num_heads = total.shape[0]
    share = num_heads // count
    lanes = local_state.shape[2]
    payload = jnp.concatenate(
        [local_state, local_source, jnp.broadcast_to(total[:, None, None], (num_heads, 1, lanes))],
        axis=1,
    )
    got = lax.all_to_all(payload, "ctx", 0, 0, tiled=True)
    got = got.reshape(count, share, got.shape[1], lanes)
    width = local_state.shape[1]
    states = got[:, :, :width].reshape(count, share, width * lanes)
    sources = got[:, :, width : 2 * width].reshape(count, share, width * lanes)
    totals = got[:, :, 2 * width, 0]
    slab = jnp.arange(count)
    between = (slab[None, :, None] < slab[None, None, :]) & (slab[None, None, :] < slab[:, None, None])
    exponent = jnp.einsum("jim,mh->jih", between.astype(jnp.float32), totals, precision=highest)
    before = slab[None, :] < slab[:, None]
    chain = jnp.where(before[:, :, None], jnp.exp(jnp.where(before[:, :, None], exponent, 0.0)), 0.0)
    entering = jnp.einsum("jih,ihx->jhx", chain, states, precision=highest)
    leaving = jnp.einsum("jkh,jhx->khx", chain, sources, precision=highest)
    back = jnp.concatenate(
        [entering.reshape(count * share, width, lanes), leaving.reshape(count * share, width, lanes)],
        axis=1,
    )
    mine = lax.all_to_all(back, "ctx", 0, 0, tiled=True)
    return mine[:, :width], mine[:, width:]


def per_device(inputs, b_proj, c_proj, dt_raw, a_log, dt_bias, d_skip, grad_out):
    params = lax.all_gather(jnp.stack([a_log, dt_bias, d_skip]), "dp", axis=1, tiled=True)
    alog_all, bias_all, skip_all = params[0], params[1], params[2]
    tokens = inputs.shape[1]
    num_heads = alog_all.shape[0]
    x = inputs[0].astype(jnp.float32).reshape(tokens, num_heads, P_SIZE)
    grad = grad_out[0].astype(jnp.float32).reshape(tokens, num_heads, P_SIZE)
    b = b_proj[0].astype(jnp.float32).reshape(tokens, G, N)
    c = c_proj[0].astype(jnp.float32).reshape(tokens, G, N)
    raw = dt_raw[0]
    total, local_state, local_source = slab_terms(x, b, c, raw, bias_all, alog_all, grad)
    entering, leaving = carry_across(total, local_state, local_source)
    _, pullback = jax.vjp(slab_scan, x, b, c, raw, bias_all, alog_all, skip_all, entering)
    gx, gb, gc, graw, gbias, galog, gskip, _ = pullback((grad, leaving))
    grad_inputs = gx.reshape(tokens, num_heads * P_SIZE).astype(jnp.bfloat16)[None]
    grad_b = gb.reshape(tokens, G * N).astype(jnp.bfloat16)[None]
    grad_c = gc.reshape(tokens, G * N).astype(jnp.bfloat16)[None]
    grad_dt = graw[None]
    head_stats = jnp.stack([galog, gbias, gskip], axis=0)
    share_size = num_heads // lax.axis_size("dp")
    summed = lax.psum(head_stats, ("ctx", "dp"))
    own_totals = lax.dynamic_slice_in_dim(summed, lax.axis_index("dp") * share_size, share_size, 1)
    return (grad_inputs, grad_b, grad_c, grad_dt, own_totals[0], own_totals[1], own_totals[2])


def solution(mesh):
    in_specs = (
        P("dp", "ctx", None),
        P("dp", "ctx", None),
        P("dp", "ctx", None),
        P("dp", None, "ctx"),
        P("dp"),
        P("dp"),
        P("dp"),
        P("dp", "ctx", None),
    )
    out_specs = (
        P("dp", "ctx", None),
        P("dp", "ctx", None),
        P("dp", "ctx", None),
        P("dp", None, "ctx"),
        P("dp"),
        P("dp"),
        P("dp"),
    )
    return jax.shard_map(
        per_device, mesh=mesh, in_specs=in_specs, out_specs=out_specs, check_vma=False
    )
```

```python
import jax
import jax.numpy as jnp
from jax import lax
from jax.sharding import PartitionSpec as P

P_SIZE = 64
N = 64
G = 8


highest = lax.Precision.HIGHEST


def slab_scan(x, b, c, raw, bias, alog, skip, state_in):
    tokens, num_heads, width = x.shape
    group_heads = num_heads // G
    dt_value = jax.nn.softplus(raw + bias[:, None])
    log_decay = dt_value * (-jnp.exp(alog))[:, None]
    cumulative = jnp.cumsum(log_decay, axis=1)
    scaled = (x * dt_value.T[:, :, None]).reshape(tokens, G, group_heads, width)
    scores = jnp.einsum("qgn,kgn->gqk", c, b, precision=highest)
    offsets = jnp.arange(tokens)
    causal = offsets[:, None] >= offsets[None, :]
    spread = cumulative[:, :, None] - cumulative[:, None, :]
    weights = jnp.where(causal, jnp.exp(jnp.where(causal, spread, 0.0)), 0.0)
    mixed = weights.reshape(G, group_heads, tokens, tokens) * scores[:, None]
    local_part = jnp.einsum("gjqk,kgjp->qgjp", mixed, scaled, precision=highest)
    tail_decay = jnp.exp(cumulative[:, -1:] - cumulative)
    weighted_b = b[:, :, None, :] * tail_decay.T.reshape(tokens, G, group_heads)[:, :, :, None]
    block_state = jnp.einsum("kgjn,kgjp->gjpn", weighted_b, scaled, precision=highest)
    block_state = block_state.reshape(num_heads, width, N)
    state_out = jnp.exp(cumulative[:, -1])[:, None, None] * state_in + block_state
    entering = state_in.reshape(G, group_heads, width, N)
    cross_part = jnp.einsum("qgn,gjpn->qgjp", c, entering, precision=highest)
    cross_part = cross_part * jnp.exp(cumulative).T.reshape(tokens, G, group_heads)[:, :, :, None]
    result = (local_part + cross_part).reshape(tokens, num_heads, width)
    result = result + skip[None, :, None] * x
    return (result, state_out)


def slab_terms(x, b, c, raw, bias, alog, grad):
    tokens, num_heads, width = x.shape
    group_heads = num_heads // G
    dt_value = jax.nn.softplus(raw + bias[:, None])
    log_decay = dt_value * (-jnp.exp(alog))[:, None]
    cumulative = jnp.cumsum(log_decay, axis=1)
    total = cumulative[:, -1]
    tail_decay = jnp.exp(total[:, None] - cumulative)
    carried = (x * (dt_value * tail_decay).T[:, :, None]).reshape(tokens, G, group_heads, width)
    local_state = jnp.einsum("tgn,tgjp->gjpn", b, carried, precision=highest)
    weighted_grad = (grad * jnp.exp(cumulative).T[:, :, None]).reshape(tokens, G, group_heads, width)
    local_source = jnp.einsum("tgn,tgjp->gjpn", c, weighted_grad, precision=highest)
    return (
        total,
        local_state.reshape(num_heads, width, N),
        local_source.reshape(num_heads, width, N),
    )


def carry_across(total, local_state, local_source):
    count = lax.axis_size("ctx")
    num_heads = total.shape[0]
    share = num_heads // count
    lanes = local_state.shape[2]
    payload = jnp.concatenate(
        [local_state, local_source, jnp.broadcast_to(total[:, None, None], (num_heads, 1, lanes))],
        axis=1,
    )
    got = lax.all_to_all(payload, "ctx", 0, 0, tiled=True)
    got = got.reshape(count, share, got.shape[1], lanes)
    width = local_state.shape[1]
    states = got[:, :, :width].reshape(count, share, width * lanes)
    sources = got[:, :, width : 2 * width].reshape(count, share, width * lanes)
    totals = got[:, :, 2 * width, 0]
    slab = jnp.arange(count)
    between = (slab[None, :, None] < slab[None, None, :]) & (slab[None, None, :] < slab[:, None, None])
    exponent = jnp.einsum("jim,mh->jih", between.astype(jnp.float32), totals, precision=highest)
    before = slab[None, :] < slab[:, None]
    chain = jnp.where(before[:, :, None], jnp.exp(jnp.where(before[:, :, None], exponent, 0.0)), 0.0)
    entering = jnp.einsum("jih,ihx->jhx", chain, states, precision=highest)
    leaving = jnp.einsum("jkh,jhx->khx", chain, sources, precision=highest)
    back = jnp.concatenate(
        [entering.reshape(count * share, width, lanes), leaving.reshape(count * share, width, lanes)],
        axis=1,
    )
    mine = lax.all_to_all(back, "ctx", 0, 0, tiled=True)
    return mine[:, :width], mine[:, width:]


def exchange(value, axis, distance):
    count = lax.axis_size(axis)
    return lax.ppermute(value, axis, [(i, i ^ distance) for i in range(count)])


def gather_by_doubling(value, axis):
    count = lax.axis_size(axis)
    place = lax.axis_index(axis)
    distance = 1
    while distance < count:
        other = exchange(value, axis, distance)
        upper = (place & distance) != 0
        value = jnp.where(
            upper,
            jnp.concatenate([other, value], axis=-1),
            jnp.concatenate([value, other], axis=-1),
        )
        distance *= 2
    return value


def sum_by_butterfly(value, axes):
    for axis in axes:
        distance = 1
        while distance < lax.axis_size(axis):
            value = value + exchange(value, axis, distance)
            distance *= 2
    return value


def per_device(inputs, b_proj, c_proj, dt_raw, a_log, dt_bias, d_skip, grad_out):
    params = gather_by_doubling(jnp.stack([a_log, dt_bias, d_skip]), "dp")
    alog_all, bias_all, skip_all = params[0], params[1], params[2]
    tokens = inputs.shape[1]
    num_heads = alog_all.shape[0]
    x = inputs[0].astype(jnp.float32).reshape(tokens, num_heads, P_SIZE)
    grad = grad_out[0].astype(jnp.float32).reshape(tokens, num_heads, P_SIZE)
    b = b_proj[0].astype(jnp.float32).reshape(tokens, G, N)
    c = c_proj[0].astype(jnp.float32).reshape(tokens, G, N)
    raw = dt_raw[0]
    total, local_state, local_source = slab_terms(x, b, c, raw, bias_all, alog_all, grad)
    entering, leaving = carry_across(total, local_state, local_source)
    _, pullback = jax.vjp(slab_scan, x, b, c, raw, bias_all, alog_all, skip_all, entering)
    gx, gb, gc, graw, gbias, galog, gskip, _ = pullback((grad, leaving))
    grad_inputs = gx.reshape(tokens, num_heads * P_SIZE).astype(jnp.bfloat16)[None]
    grad_b = gb.reshape(tokens, G * N).astype(jnp.bfloat16)[None]
    grad_c = gc.reshape(tokens, G * N).astype(jnp.bfloat16)[None]
    grad_dt = graw[None]
    head_stats = jnp.stack([galog, gbias, gskip], axis=0)
    share_size = num_heads // lax.axis_size("dp")
    summed = sum_by_butterfly(head_stats, ("dp", "ctx"))
    own_totals = lax.dynamic_slice_in_dim(summed, lax.axis_index("dp") * share_size, share_size, 1)
    return (grad_inputs, grad_b, grad_c, grad_dt, own_totals[0], own_totals[1], own_totals[2])


def solution(mesh):
    in_specs = (
        P("dp", "ctx", None),
        P("dp", "ctx", None),
        P("dp", "ctx", None),
        P("dp", None, "ctx"),
        P("dp"),
        P("dp"),
        P("dp"),
        P("dp", "ctx", None),
    )
    out_specs = (
        P("dp", "ctx", None),
        P("dp", "ctx", None),
        P("dp", "ctx", None),
        P("dp", None, "ctx"),
        P("dp"),
        P("dp"),
        P("dp"),
    )
    return jax.shard_map(
        per_device, mesh=mesh, in_specs=in_specs, out_specs=out_specs, check_vma=False
    )
```

```python
import jax
import jax.numpy as jnp
from jax import lax
from jax.sharding import PartitionSpec as P

P_SIZE = 64
N = 64
G = 8


highest = lax.Precision.HIGHEST


def slab_prelude(x, raw, bias, alog):
    tokens, num_heads, width = x.shape
    dt_value = jax.nn.softplus(raw + bias[:, None])
    log_decay = dt_value * (-jnp.exp(alog))[:, None]
    cumulative = jnp.cumsum(log_decay, axis=1)
    scaled = (x * dt_value.T[:, :, None]).reshape(tokens, G, num_heads // G, width)
    return cumulative, scaled


def slab_local(x, b, c, raw, bias, alog, skip):
    tokens, num_heads, width = x.shape
    group_heads = num_heads // G
    cumulative, scaled = slab_prelude(x, raw, bias, alog)
    scores = jnp.einsum("qgn,kgn->gqk", c, b, precision=highest)
    offsets = jnp.arange(tokens)
    causal = offsets[:, None] >= offsets[None, :]
    spread = cumulative[:, :, None] - cumulative[:, None, :]
    weights = jnp.where(causal, jnp.exp(jnp.where(causal, spread, 0.0)), 0.0)
    mixed = weights.reshape(G, group_heads, tokens, tokens) * scores[:, None]
    local_part = jnp.einsum("gjqk,kgjp->qgjp", mixed, scaled, precision=highest)
    return local_part.reshape(tokens, num_heads, width) + skip[None, :, None] * x


def slab_carry(x, b, c, raw, bias, alog, state_in):
    tokens, num_heads, width = x.shape
    group_heads = num_heads // G
    cumulative, scaled = slab_prelude(x, raw, bias, alog)
    tail_decay = jnp.exp(cumulative[:, -1:] - cumulative)
    weighted_b = b[:, :, None, :] * tail_decay.T.reshape(tokens, G, group_heads)[:, :, :, None]
    block_state = jnp.einsum("kgjn,kgjp->gjpn", weighted_b, scaled, precision=highest)
    block_state = block_state.reshape(num_heads, width, N)
    state_out = jnp.exp(cumulative[:, -1])[:, None, None] * state_in + block_state
    entering = state_in.reshape(G, group_heads, width, N)
    cross_part = jnp.einsum("qgn,gjpn->qgjp", c, entering, precision=highest)
    cross_part = cross_part * jnp.exp(cumulative).T.reshape(tokens, G, group_heads)[:, :, :, None]
    return (cross_part.reshape(tokens, num_heads, width), state_out)


def slab_terms(x, b, c, raw, bias, alog, grad):
    tokens, num_heads, width = x.shape
    group_heads = num_heads // G
    dt_value = jax.nn.softplus(raw + bias[:, None])
    log_decay = dt_value * (-jnp.exp(alog))[:, None]
    cumulative = jnp.cumsum(log_decay, axis=1)
    total = cumulative[:, -1]
    tail_decay = jnp.exp(total[:, None] - cumulative)
    carried = (x * (dt_value * tail_decay).T[:, :, None]).reshape(tokens, G, group_heads, width)
    local_state = jnp.einsum("tgn,tgjp->gjpn", b, carried, precision=highest)
    weighted_grad = (grad * jnp.exp(cumulative).T[:, :, None]).reshape(tokens, G, group_heads, width)
    local_source = jnp.einsum("tgn,tgjp->gjpn", c, weighted_grad, precision=highest)
    return (
        total,
        local_state.reshape(num_heads, width, N),
        local_source.reshape(num_heads, width, N),
    )


def carry_across(total, local_state, local_source, held):
    count = lax.axis_size("ctx")
    num_heads, width, lanes = local_state.shape
    share = num_heads // count
    rows = width * lanes // 128
    block = share * rows
    states = local_state.reshape(count, block, 128)
    sources = local_source.reshape(count, block, 128)
    totals = jnp.broadcast_to(total.reshape(count, share, 1), (count, share, 128))
    padding = -share % 8
    if padding:
        totals = jnp.concatenate([totals, jnp.zeros((count, padding, 128), totals.dtype)], axis=1)
    payload = jnp.concatenate([states, sources, totals], axis=1)
    chunk = payload.shape[1]
    got = lax.all_to_all(payload.reshape(count * chunk, 128), "ctx", 0, 0, tiled=True)
    got, held = lax.optimization_barrier((got, held))
    got = got.reshape(count, chunk, 128)
    states = got[:, :block].reshape(count * share, rows, 128)
    sources = got[:, block : 2 * block].reshape(count * share, rows, 128)
    totals = got[:, 2 * block : 2 * block + share, 0]
    slab = jnp.arange(count)
    between = (slab[None, :, None] < slab[None, None, :]) & (slab[None, None, :] < slab[:, None, None])
    exponent = jnp.einsum("jim,mh->jih", between.astype(jnp.float32), totals, precision=highest)
    before = slab[None, :] < slab[:, None]
    chain = jnp.where(before[:, :, None], jnp.exp(jnp.where(before[:, :, None], exponent, 0.0)), 0.0)
    same = jnp.eye(share, dtype=chain.dtype)
    spread = (chain[:, :, :, None] * same[None, None]).transpose(0, 2, 1, 3)
    spread = spread.reshape(count * share, count * share)
    entering = jnp.einsum("ab,brl->arl", spread, states, precision=highest)
    leaving = jnp.einsum("ba,brl->arl", spread, sources, precision=highest)
    back = jnp.concatenate(
        [entering.reshape(count, block, 128), leaving.reshape(count, block, 128)], axis=1
    )
    mine = lax.all_to_all(back.reshape(count * 2 * block, 128), "ctx", 0, 0, tiled=True)
    mine = mine.reshape(count, 2 * block, 128)
    entering = mine[:, :block].reshape(num_heads, width, lanes)
    leaving = mine[:, block:].reshape(num_heads, width, lanes)
    return entering, leaving, held


def exchange(value, axis, distance):
    count = lax.axis_size(axis)
    return lax.ppermute(value, axis, [(i, i ^ distance) for i in range(count)])


def gather_by_doubling(value, axis):
    count = lax.axis_size(axis)
    place = lax.axis_index(axis)
    distance = 1
    while distance < count:
        other = exchange(value, axis, distance)
        upper = (place & distance) != 0
        value = jnp.where(
            upper,
            jnp.concatenate([other, value], axis=-1),
            jnp.concatenate([value, other], axis=-1),
        )
        distance *= 2
    return value


def sum_by_butterfly(value, axes):
    for axis in axes:
        distance = 1
        while distance < lax.axis_size(axis):
            value = value + exchange(value, axis, distance)
            distance *= 2
    return value


def per_device(inputs, b_proj, c_proj, dt_raw, a_log, dt_bias, d_skip, grad_out):
    params = gather_by_doubling(jnp.stack([a_log, dt_bias, d_skip]), "dp")
    alog_all, bias_all, skip_all = params[0], params[1], params[2]
    tokens = inputs.shape[1]
    num_heads = alog_all.shape[0]
    x = inputs[0].astype(jnp.float32).reshape(tokens, num_heads, P_SIZE)
    grad = grad_out[0].astype(jnp.float32).reshape(tokens, num_heads, P_SIZE)
    b = b_proj[0].astype(jnp.float32).reshape(tokens, G, N)
    c = c_proj[0].astype(jnp.float32).reshape(tokens, G, N)
    raw = dt_raw[0]
    total, local_state, local_source = slab_terms(x, b, c, raw, bias_all, alog_all, grad)
    (total, local_state, local_source), late = lax.optimization_barrier(
        ((total, local_state, local_source), (x, b, c, raw, bias_all, alog_all, skip_all, grad))
    )
    _, local_pullback = jax.vjp(slab_local, *late[:7])
    local_grads = local_pullback(late[7])
    entering, leaving, local_grads = carry_across(total, local_state, local_source, local_grads)
    _, carry_pullback = jax.vjp(slab_carry, x, b, c, raw, bias_all, alog_all, entering)
    carry_grads = carry_pullback((grad, leaving))[:6]
    gx, gb, gc, graw, gbias, galog = [u + v for u, v in zip(local_grads[:6], carry_grads)]
    gskip = local_grads[6]
    grad_inputs = gx.reshape(tokens, num_heads * P_SIZE).astype(jnp.bfloat16)[None]
    grad_b = gb.reshape(tokens, G * N).astype(jnp.bfloat16)[None]
    grad_c = gc.reshape(tokens, G * N).astype(jnp.bfloat16)[None]
    grad_dt = graw[None]
    head_stats = jnp.stack([galog, gbias, gskip], axis=0)
    share_size = num_heads // lax.axis_size("dp")
    summed = sum_by_butterfly(head_stats, ("dp", "ctx"))
    own_totals = lax.dynamic_slice_in_dim(summed, lax.axis_index("dp") * share_size, share_size, 1)
    return (grad_inputs, grad_b, grad_c, grad_dt, own_totals[0], own_totals[1], own_totals[2])


def solution(mesh):
    in_specs = (
        P("dp", "ctx", None),
        P("dp", "ctx", None),
        P("dp", "ctx", None),
        P("dp", None, "ctx"),
        P("dp"),
        P("dp"),
        P("dp"),
        P("dp", "ctx", None),
    )
    out_specs = (
        P("dp", "ctx", None),
        P("dp", "ctx", None),
        P("dp", "ctx", None),
        P("dp", None, "ctx"),
        P("dp"),
        P("dp"),
        P("dp"),
    )
    return jax.shard_map(
        per_device, mesh=mesh, in_specs=in_specs, out_specs=out_specs, check_vma=False
    )
```

```python
import jax
import jax.numpy as jnp
from jax import lax
from jax.sharding import PartitionSpec as P

P_SIZE = 64
N = 64
G = 8


highest = lax.Precision.HIGHEST


def slab_prelude(x, raw, bias, alog):
    tokens, num_heads, width = x.shape
    dt_value = jax.nn.softplus(raw + bias[:, None])
    log_decay = dt_value * (-jnp.exp(alog))[:, None]
    cumulative = jnp.cumsum(log_decay, axis=1)
    scaled = (x * dt_value.T[:, :, None]).reshape(tokens, G, num_heads // G, width)
    return cumulative, scaled


def slab_local(x, b, c, raw, bias, alog, skip):
    tokens, num_heads, width = x.shape
    group_heads = num_heads // G
    cumulative, scaled = slab_prelude(x, raw, bias, alog)
    scores = jnp.einsum("qgn,kgn->gqk", c, b, precision=highest)
    offsets = jnp.arange(tokens)
    causal = offsets[:, None] >= offsets[None, :]
    spread = cumulative[:, :, None] - cumulative[:, None, :]
    weights = jnp.where(causal, jnp.exp(jnp.where(causal, spread, 0.0)), 0.0)
    mixed = weights.reshape(G, group_heads, tokens, tokens) * scores[:, None]
    local_part = jnp.einsum("gjqk,kgjp->qgjp", mixed, scaled, precision=highest)
    return local_part.reshape(tokens, num_heads, width) + skip[None, :, None] * x


def slab_carry(x, b, c, raw, bias, alog, state_in):
    tokens, num_heads, width = x.shape
    group_heads = num_heads // G
    cumulative, scaled = slab_prelude(x, raw, bias, alog)
    tail_decay = jnp.exp(cumulative[:, -1:] - cumulative)
    weighted_b = b[:, :, None, :] * tail_decay.T.reshape(tokens, G, group_heads)[:, :, :, None]
    block_state = jnp.einsum("kgjn,kgjp->gjpn", weighted_b, scaled, precision=highest)
    block_state = block_state.reshape(num_heads, width, N)
    state_out = jnp.exp(cumulative[:, -1])[:, None, None] * state_in + block_state
    entering = state_in.reshape(G, group_heads, width, N)
    cross_part = jnp.einsum("qgn,gjpn->qgjp", c, entering, precision=highest)
    cross_part = cross_part * jnp.exp(cumulative).T.reshape(tokens, G, group_heads)[:, :, :, None]
    return (cross_part.reshape(tokens, num_heads, width), state_out)


def slab_terms(x, b, c, raw, bias, alog, grad):
    tokens, num_heads, width = x.shape
    group_heads = num_heads // G
    dt_value = jax.nn.softplus(raw + bias[:, None])
    log_decay = dt_value * (-jnp.exp(alog))[:, None]
    cumulative = jnp.cumsum(log_decay, axis=1)
    total = cumulative[:, -1]
    tail_decay = jnp.exp(total[:, None] - cumulative)
    carried = (x * (dt_value * tail_decay).T[:, :, None]).reshape(tokens, G, group_heads, width)
    local_state = jnp.einsum("tgn,tgjp->gjpn", b, carried, precision=highest)
    weighted_grad = (grad * jnp.exp(cumulative).T[:, :, None]).reshape(tokens, G, group_heads, width)
    local_source = jnp.einsum("tgn,tgjp->gjpn", c, weighted_grad, precision=highest)
    return (
        total,
        local_state.reshape(num_heads, width, N),
        local_source.reshape(num_heads, width, N),
    )


def carry_across(total, local_state, local_source, held):
    count = lax.axis_size("ctx")
    num_heads, width, lanes = local_state.shape
    share = num_heads // count
    rows = width * lanes // 128
    block = share * rows
    states = local_state.reshape(count, block, 128)
    sources = local_source.reshape(count, block, 128)
    totals = jnp.broadcast_to(total.reshape(count, share, 1), (count, share, 128))
    padding = -share % 8
    if padding:
        totals = jnp.concatenate([totals, jnp.zeros((count, padding, 128), totals.dtype)], axis=1)
    payload = jnp.concatenate([states, sources, totals], axis=1)
    chunk = payload.shape[1]
    got = lax.all_to_all(payload.reshape(count * chunk, 128), "ctx", 0, 0, tiled=True)
    got, held = lax.optimization_barrier((got, held))
    got = got.reshape(count, chunk, 128)
    states = got[:, :block].reshape(count * share, rows, 128)
    sources = got[:, block : 2 * block].reshape(count * share, rows, 128)
    totals = got[:, 2 * block : 2 * block + share, 0]
    slab = jnp.arange(count)
    between = (slab[None, :, None] < slab[None, None, :]) & (slab[None, None, :] < slab[:, None, None])
    exponent = jnp.einsum("jim,mh->jih", between.astype(jnp.float32), totals, precision=highest)
    before = slab[None, :] < slab[:, None]
    chain = jnp.where(before[:, :, None], jnp.exp(jnp.where(before[:, :, None], exponent, 0.0)), 0.0)
    same = jnp.eye(share, dtype=chain.dtype)
    spread = (chain[:, :, :, None] * same[None, None]).transpose(0, 2, 1, 3)
    spread = spread.reshape(count * share, count * share)
    entering = jnp.einsum("ab,brl->arl", spread, states, precision=highest)
    leaving = jnp.einsum("ba,brl->arl", spread, sources, precision=highest)
    back = jnp.concatenate(
        [entering.reshape(count, block, 128), leaving.reshape(count, block, 128)], axis=1
    )
    mine = lax.all_to_all(back.reshape(count * 2 * block, 128), "ctx", 0, 0, tiled=True)
    mine = mine.reshape(count, 2 * block, 128)
    entering = mine[:, :block].reshape(num_heads, width, lanes)
    leaving = mine[:, block:].reshape(num_heads, width, lanes)
    return entering, leaving, held


def exchange(value, axis, distance):
    count = lax.axis_size(axis)
    return lax.ppermute(value, axis, [(i, i ^ distance) for i in range(count)])


def group_values(value, axis, stride):
    place = (lax.axis_index(axis) // stride) % 4
    held = [value] + [exchange(value, axis, step * stride) for step in (1, 2, 3)]
    ordered = []
    for position in range(4):
        pick = held[3]
        for step in (2, 1, 0):
            pick = jnp.where((place ^ step) == position, held[step], pick)
        ordered.append(pick)
    return ordered


def gather_by_doubling(value, axis):
    stride = 1
    while stride < lax.axis_size(axis):
        value = jnp.concatenate(group_values(value, axis, stride), axis=-1)
        stride *= 4
    return value


def sum_by_butterfly(value, axes):
    for axis in axes:
        stride = 1
        while stride < lax.axis_size(axis):
            first, second, third, fourth = group_values(value, axis, stride)
            value = (first + second) + (third + fourth)
            stride *= 4
    return value


def per_device(inputs, b_proj, c_proj, dt_raw, a_log, dt_bias, d_skip, grad_out):
    params = gather_by_doubling(jnp.stack([a_log, dt_bias, d_skip]), "dp")
    alog_all, bias_all, skip_all = params[0], params[1], params[2]
    tokens = inputs.shape[1]
    num_heads = alog_all.shape[0]
    x = inputs[0].astype(jnp.float32).reshape(tokens, num_heads, P_SIZE)
    grad = grad_out[0].astype(jnp.float32).reshape(tokens, num_heads, P_SIZE)
    b = b_proj[0].astype(jnp.float32).reshape(tokens, G, N)
    c = c_proj[0].astype(jnp.float32).reshape(tokens, G, N)
    raw = dt_raw[0]
    total, local_state, local_source = slab_terms(x, b, c, raw, bias_all, alog_all, grad)
    (total, local_state, local_source), late = lax.optimization_barrier(
        ((total, local_state, local_source), (x, b, c, raw, bias_all, alog_all, skip_all, grad))
    )
    _, local_pullback = jax.vjp(slab_local, *late[:7])
    local_grads = local_pullback(late[7])
    entering, leaving, local_grads = carry_across(total, local_state, local_source, local_grads)
    _, carry_pullback = jax.vjp(slab_carry, x, b, c, raw, bias_all, alog_all, entering)
    carry_grads = carry_pullback((grad, leaving))[:6]
    gx, gb, gc, graw, gbias, galog = [u + v for u, v in zip(local_grads[:6], carry_grads)]
    gskip = local_grads[6]
    grad_inputs = gx.reshape(tokens, num_heads * P_SIZE).astype(jnp.bfloat16)[None]
    grad_b = gb.reshape(tokens, G * N).astype(jnp.bfloat16)[None]
    grad_c = gc.reshape(tokens, G * N).astype(jnp.bfloat16)[None]
    grad_dt = graw[None]
    head_stats = jnp.stack([galog, gbias, gskip], axis=0)
    share_size = num_heads // lax.axis_size("dp")
    summed = sum_by_butterfly(head_stats, ("dp", "ctx"))
    own_totals = lax.dynamic_slice_in_dim(summed, lax.axis_index("dp") * share_size, share_size, 1)
    return (grad_inputs, grad_b, grad_c, grad_dt, own_totals[0], own_totals[1], own_totals[2])


def solution(mesh):
    in_specs = (
        P("dp", "ctx", None),
        P("dp", "ctx", None),
        P("dp", "ctx", None),
        P("dp", None, "ctx"),
        P("dp"),
        P("dp"),
        P("dp"),
        P("dp", "ctx", None),
    )
    out_specs = (
        P("dp", "ctx", None),
        P("dp", "ctx", None),
        P("dp", "ctx", None),
        P("dp", None, "ctx"),
        P("dp"),
        P("dp"),
        P("dp"),
    )
    return jax.shard_map(
        per_device, mesh=mesh, in_specs=in_specs, out_specs=out_specs, check_vma=False
    )
```

```python
import jax
import jax.numpy as jnp
from jax import lax
from jax.sharding import PartitionSpec as P

P_SIZE = 64
N = 64
G = 8


highest = lax.Precision.HIGHEST


def slab_prelude(x, raw, bias, alog, groups):
    tokens, num_heads, width = x.shape
    dt_value = jax.nn.softplus(raw + bias[:, None])
    log_decay = dt_value * (-jnp.exp(alog))[:, None]
    cumulative = jnp.cumsum(log_decay, axis=1)
    scaled = (x * dt_value.T[:, :, None]).reshape(tokens, groups, num_heads // groups, width)
    return cumulative, scaled


def slab_local(x, b, c, raw, bias, alog, skip):
    tokens, num_heads, width = x.shape
    G = b.shape[1]
    group_heads = num_heads // G
    cumulative, scaled = slab_prelude(x, raw, bias, alog, G)
    scores = jnp.einsum("qgn,kgn->gqk", c, b, precision=highest)
    offsets = jnp.arange(tokens)
    causal = offsets[:, None] >= offsets[None, :]
    spread = cumulative[:, :, None] - cumulative[:, None, :]
    weights = jnp.where(causal, jnp.exp(jnp.where(causal, spread, 0.0)), 0.0)
    mixed = weights.reshape(G, group_heads, tokens, tokens) * scores[:, None]
    local_part = jnp.einsum("gjqk,kgjp->qgjp", mixed, scaled, precision=highest)
    return local_part.reshape(tokens, num_heads, width) + skip[None, :, None] * x


def slab_carry(x, b, c, raw, bias, alog, state_in):
    tokens, num_heads, width = x.shape
    G = b.shape[1]
    group_heads = num_heads // G
    cumulative, scaled = slab_prelude(x, raw, bias, alog, G)
    tail_decay = jnp.exp(cumulative[:, -1:] - cumulative)
    weighted_b = b[:, :, None, :] * tail_decay.T.reshape(tokens, G, group_heads)[:, :, :, None]
    block_state = jnp.einsum("kgjn,kgjp->gjpn", weighted_b, scaled, precision=highest)
    block_state = block_state.reshape(num_heads, width, N)
    state_out = jnp.exp(cumulative[:, -1])[:, None, None] * state_in + block_state
    entering = state_in.reshape(G, group_heads, width, N)
    cross_part = jnp.einsum("qgn,gjpn->qgjp", c, entering, precision=highest)
    cross_part = cross_part * jnp.exp(cumulative).T.reshape(tokens, G, group_heads)[:, :, :, None]
    return (cross_part.reshape(tokens, num_heads, width), state_out)


def slab_terms(x, b, c, raw, bias, alog, grad):
    tokens, num_heads, width = x.shape
    group_heads = num_heads // G
    dt_value = jax.nn.softplus(raw + bias[:, None])
    log_decay = dt_value * (-jnp.exp(alog))[:, None]
    cumulative = jnp.cumsum(log_decay, axis=1)
    total = cumulative[:, -1]
    tail_decay = jnp.exp(total[:, None] - cumulative)
    carried = (x * (dt_value * tail_decay).T[:, :, None]).reshape(tokens, G, group_heads, width)
    local_state = jnp.einsum("tgn,tgjp->gjpn", b, carried, precision=highest)
    weighted_grad = (grad * jnp.exp(cumulative).T[:, :, None]).reshape(tokens, G, group_heads, width)
    local_source = jnp.einsum("tgn,tgjp->gjpn", c, weighted_grad, precision=highest)
    return (
        total,
        local_state.reshape(num_heads, width, N),
        local_source.reshape(num_heads, width, N),
    )


def carry_across(total, local_state, local_source, held):
    count = lax.axis_size("ctx")
    num_heads, width, lanes = local_state.shape
    share = num_heads // count
    rows = width * lanes // 128
    block = share * rows
    states = local_state.reshape(count, block, 128)
    sources = local_source.reshape(count, block, 128)
    totals = jnp.broadcast_to(total.reshape(count, share, 1), (count, share, 128))
    padding = -share % 8
    if padding:
        totals = jnp.concatenate([totals, jnp.zeros((count, padding, 128), totals.dtype)], axis=1)
    payload = jnp.concatenate([states, sources, totals], axis=1)
    chunk = payload.shape[1]
    got = lax.all_to_all(payload.reshape(count * chunk, 128), "ctx", 0, 0, tiled=True)
    got, held = lax.optimization_barrier((got, held))
    got = got.reshape(count, chunk, 128)
    states = got[:, :block].reshape(count * share, rows, 128)
    sources = got[:, block : 2 * block].reshape(count * share, rows, 128)
    totals = got[:, 2 * block : 2 * block + share, 0]
    slab = jnp.arange(count)
    between = (slab[None, :, None] < slab[None, None, :]) & (slab[None, None, :] < slab[:, None, None])
    exponent = jnp.einsum("jim,mh->jih", between.astype(jnp.float32), totals, precision=highest)
    before = slab[None, :] < slab[:, None]
    chain = jnp.where(before[:, :, None], jnp.exp(jnp.where(before[:, :, None], exponent, 0.0)), 0.0)
    same = jnp.eye(share, dtype=chain.dtype)
    spread = (chain[:, :, :, None] * same[None, None]).transpose(0, 2, 1, 3)
    spread = spread.reshape(count * share, count * share)
    entering = jnp.einsum("ab,brl->arl", spread, states, precision=highest)
    leaving = jnp.einsum("ba,brl->arl", spread, sources, precision=highest)
    back = jnp.concatenate(
        [entering.reshape(count, block, 128), leaving.reshape(count, block, 128)], axis=1
    )
    mine = lax.all_to_all(back.reshape(count * 2 * block, 128), "ctx", 0, 0, tiled=True)
    mine = mine.reshape(count, 2 * block, 128)
    entering = mine[:, :block].reshape(num_heads, width, lanes)
    leaving = mine[:, block:].reshape(num_heads, width, lanes)
    return entering, leaving, held


def exchange(value, axis, distance):
    count = lax.axis_size(axis)
    return lax.ppermute(value, axis, [(i, i ^ distance) for i in range(count)])


def group_values(value, axis, stride):
    place = (lax.axis_index(axis) // stride) % 4
    held = [value] + [exchange(value, axis, step * stride) for step in (1, 2, 3)]
    ordered = []
    for position in range(4):
        pick = held[3]
        for step in (2, 1, 0):
            pick = jnp.where((place ^ step) == position, held[step], pick)
        ordered.append(pick)
    return ordered


def gather_by_doubling(value, axis):
    stride = 1
    while stride < lax.axis_size(axis):
        value = jnp.concatenate(group_values(value, axis, stride), axis=-1)
        stride *= 4
    return value


def sum_by_butterfly(value, axes):
    for axis in axes:
        stride = 1
        while stride < lax.axis_size(axis):
            first, second, third, fourth = group_values(value, axis, stride)
            value = (first + second) + (third + fourth)
            stride *= 4
    return value


def per_device(inputs, b_proj, c_proj, dt_raw, a_log, dt_bias, d_skip, grad_out):
    params = gather_by_doubling(jnp.stack([a_log, dt_bias, d_skip]), "dp")
    alog_all, bias_all, skip_all = params[0], params[1], params[2]
    tokens = inputs.shape[1]
    num_heads = alog_all.shape[0]
    x = inputs[0].astype(jnp.float32).reshape(tokens, num_heads, P_SIZE)
    grad = grad_out[0].astype(jnp.float32).reshape(tokens, num_heads, P_SIZE)
    b = b_proj[0].astype(jnp.float32).reshape(tokens, G, N)
    c = c_proj[0].astype(jnp.float32).reshape(tokens, G, N)
    raw = dt_raw[0]
    total, local_state, local_source = slab_terms(x, b, c, raw, bias_all, alog_all, grad)
    (total, local_state, local_source), late = lax.optimization_barrier(
        ((total, local_state, local_source), (x, b, c, raw, bias_all, alog_all, skip_all, grad))
    )
    _, local_pullback = jax.vjp(slab_local, *late[:7])
    local_grads = local_pullback(late[7])
    halves = 2
    head_part = num_heads // halves
    group_part = G // halves
    carry_parts = []
    for half in range(halves):
        heads = slice(half * head_part, (half + 1) * head_part)
        groups = slice(half * group_part, (half + 1) * group_part)
        entering, leaving, held = carry_across(
            total[heads], local_state[heads], local_source[heads], local_grads if half else ()
        )
        if half:
            local_grads = held
        _, carry_pullback = jax.vjp(
            slab_carry, x[:, heads], b[:, groups], c[:, groups], raw[heads], bias_all[heads], alog_all[heads], entering
        )
        carry_parts.append(carry_pullback((grad[:, heads], leaving))[:6])
    joined = [jnp.concatenate(parts, axis=axis) for parts, axis in zip(zip(*carry_parts), (1, 1, 1, 0, 0, 0))]
    gx, gb, gc, graw, gbias, galog = [u + v for u, v in zip(local_grads[:6], joined)]
    gskip = local_grads[6]
    grad_inputs = gx.reshape(tokens, num_heads * P_SIZE).astype(jnp.bfloat16)[None]
    grad_b = gb.reshape(tokens, G * N).astype(jnp.bfloat16)[None]
    grad_c = gc.reshape(tokens, G * N).astype(jnp.bfloat16)[None]
    grad_dt = graw[None]
    head_stats = jnp.stack([galog, gbias, gskip], axis=0)
    share_size = num_heads // lax.axis_size("dp")
    summed = sum_by_butterfly(head_stats, ("dp", "ctx"))
    own_totals = lax.dynamic_slice_in_dim(summed, lax.axis_index("dp") * share_size, share_size, 1)
    return (grad_inputs, grad_b, grad_c, grad_dt, own_totals[0], own_totals[1], own_totals[2])


def solution(mesh):
    in_specs = (
        P("dp", "ctx", None),
        P("dp", "ctx", None),
        P("dp", "ctx", None),
        P("dp", None, "ctx"),
        P("dp"),
        P("dp"),
        P("dp"),
        P("dp", "ctx", None),
    )
    out_specs = (
        P("dp", "ctx", None),
        P("dp", "ctx", None),
        P("dp", "ctx", None),
        P("dp", None, "ctx"),
        P("dp"),
        P("dp"),
        P("dp"),
    )
    return jax.shard_map(
        per_device, mesh=mesh, in_specs=in_specs, out_specs=out_specs, check_vma=False
    )
```

```python
import jax
import jax.numpy as jnp
from jax import lax
from jax.sharding import PartitionSpec as P

P_SIZE = 64
N = 64
G = 8


highest = lax.Precision.HIGHEST


def slab_prelude(x, raw, bias, alog):
    tokens, num_heads, width = x.shape
    dt_value = jax.nn.softplus(raw + bias[:, None])
    log_decay = dt_value * (-jnp.exp(alog))[:, None]
    cumulative = jnp.cumsum(log_decay, axis=1)
    scaled = (x * dt_value.T[:, :, None]).reshape(tokens, G, num_heads // G, width)
    return cumulative, scaled


def slab_local(x, b, c, raw, bias, alog, skip):
    tokens, num_heads, width = x.shape
    group_heads = num_heads // G
    cumulative, scaled = slab_prelude(x, raw, bias, alog)
    scores = jnp.einsum("qgn,kgn->gqk", c, b, precision=highest)
    offsets = jnp.arange(tokens)
    causal = offsets[:, None] >= offsets[None, :]
    spread = cumulative[:, :, None] - cumulative[:, None, :]
    weights = jnp.where(causal, jnp.exp(jnp.where(causal, spread, 0.0)), 0.0)
    mixed = weights.reshape(G, group_heads, tokens, tokens) * scores[:, None]
    local_part = jnp.einsum("gjqk,kgjp->qgjp", mixed, scaled, precision=highest)
    return local_part.reshape(tokens, num_heads, width) + skip[None, :, None] * x


def slab_carry(x, b, c, raw, bias, alog, state_in):
    tokens, num_heads, width = x.shape
    group_heads = num_heads // G
    cumulative, scaled = slab_prelude(x, raw, bias, alog)
    tail_decay = jnp.exp(cumulative[:, -1:] - cumulative)
    weighted_b = b[:, :, None, :] * tail_decay.T.reshape(tokens, G, group_heads)[:, :, :, None]
    block_state = jnp.einsum("kgjn,kgjp->gjpn", weighted_b, scaled, precision=highest)
    block_state = block_state.reshape(num_heads, width, N)
    state_out = jnp.exp(cumulative[:, -1])[:, None, None] * state_in + block_state
    entering = state_in.reshape(G, group_heads, width, N)
    cross_part = jnp.einsum("qgn,gjpn->qgjp", c, entering, precision=highest)
    cross_part = cross_part * jnp.exp(cumulative).T.reshape(tokens, G, group_heads)[:, :, :, None]
    return (cross_part.reshape(tokens, num_heads, width), state_out)


def slab_terms(x, b, c, raw, bias, alog, grad):
    tokens, num_heads, width = x.shape
    group_heads = num_heads // G
    dt_value = jax.nn.softplus(raw + bias[:, None])
    log_decay = dt_value * (-jnp.exp(alog))[:, None]
    cumulative = jnp.cumsum(log_decay, axis=1)
    total = cumulative[:, -1]
    tail_decay = jnp.exp(total[:, None] - cumulative)
    carried = (x * (dt_value * tail_decay).T[:, :, None]).reshape(tokens, G, group_heads, width)
    local_state = jnp.einsum("tgn,tgjp->gjpn", b, carried, precision=highest)
    weighted_grad = (grad * jnp.exp(cumulative).T[:, :, None]).reshape(tokens, G, group_heads, width)
    local_source = jnp.einsum("tgn,tgjp->gjpn", c, weighted_grad, precision=highest)
    return (
        total,
        local_state.reshape(num_heads, width, N),
        local_source.reshape(num_heads, width, N),
    )


def carry_across(total, local_state, local_source, held):
    count = lax.axis_size("ctx")
    num_heads, width, lanes = local_state.shape
    share = num_heads // count
    rows = width * lanes // 128
    block = share * rows
    states = local_state.reshape(count, block, 128)
    sources = local_source.reshape(count, block, 128)
    totals = jnp.broadcast_to(total.reshape(count, share, 1), (count, share, 128))
    padding = -share % 8
    if padding:
        totals = jnp.concatenate([totals, jnp.zeros((count, padding, 128), totals.dtype)], axis=1)
    payload = jnp.concatenate([states, sources, totals], axis=1)
    chunk = payload.shape[1]
    got = lax.all_to_all(payload.reshape(count * chunk, 128), "ctx", 0, 0, tiled=True)
    got, held = lax.optimization_barrier((got, held))
    got = got.reshape(count, chunk, 128)
    states = got[:, :block].reshape(count * share, rows, 128)
    sources = got[:, block : 2 * block].reshape(count * share, rows, 128)
    totals = got[:, 2 * block : 2 * block + share, 0]
    slab = jnp.arange(count)
    between = (slab[None, :, None] < slab[None, None, :]) & (slab[None, None, :] < slab[:, None, None])
    exponent = jnp.einsum("jim,mh->jih", between.astype(jnp.float32), totals, precision=highest)
    before = slab[None, :] < slab[:, None]
    chain = jnp.where(before[:, :, None], jnp.exp(jnp.where(before[:, :, None], exponent, 0.0)), 0.0)
    same = jnp.eye(share, dtype=chain.dtype)
    spread = (chain[:, :, :, None] * same[None, None]).transpose(0, 2, 1, 3)
    spread = spread.reshape(count * share, count * share)
    entering = jnp.einsum("ab,brl->arl", spread, states, precision=highest)
    leaving = jnp.einsum("ba,brl->arl", spread, sources, precision=highest)
    back = jnp.concatenate(
        [entering.reshape(count, block, 128), leaving.reshape(count, block, 128)], axis=1
    )
    mine = lax.all_to_all(back.reshape(count * 2 * block, 128), "ctx", 0, 0, tiled=True)
    mine = mine.reshape(count, 2 * block, 128)
    entering = mine[:, :block].reshape(num_heads, width, lanes)
    leaving = mine[:, block:].reshape(num_heads, width, lanes)
    return entering, leaving, held


def exchange(value, axis, distance):
    count = lax.axis_size(axis)
    return lax.ppermute(value, axis, [(i, i ^ distance) for i in range(count)])


def group_values(value, axis, stride):
    place = (lax.axis_index(axis) // stride) % 4
    held = [value] + [exchange(value, axis, step * stride) for step in (1, 2, 3)]
    ordered = []
    for position in range(4):
        pick = held[3]
        for step in (2, 1, 0):
            pick = jnp.where((place ^ step) == position, held[step], pick)
        ordered.append(pick)
    return ordered


def gather_by_doubling(value, axis):
    stride = 1
    while stride < lax.axis_size(axis):
        value = jnp.concatenate(group_values(value, axis, stride), axis=-1)
        stride *= 4
    return value


def sum_by_butterfly(value, axes):
    for axis in axes:
        stride = 1
        while stride < lax.axis_size(axis):
            first, second, third, fourth = group_values(value, axis, stride)
            value = (first + second) + (third + fourth)
            stride *= 4
    return value


def per_device(inputs, b_proj, c_proj, dt_raw, a_log, dt_bias, d_skip, grad_out):
    params = gather_by_doubling(jnp.stack([a_log, dt_bias, d_skip]), "dp")
    alog_all, bias_all, skip_all = params[0], params[1], params[2]
    tokens = inputs.shape[1]
    num_heads = alog_all.shape[0]
    x = inputs[0].astype(jnp.float32).reshape(tokens, num_heads, P_SIZE)
    grad = grad_out[0].astype(jnp.float32).reshape(tokens, num_heads, P_SIZE)
    b = b_proj[0].astype(jnp.float32).reshape(tokens, G, N)
    c = c_proj[0].astype(jnp.float32).reshape(tokens, G, N)
    raw = dt_raw[0]
    total, local_state, local_source = slab_terms(x, b, c, raw, bias_all, alog_all, grad)
    (total, local_state, local_source), late = lax.optimization_barrier(
        ((total, local_state, local_source), (x, b, c, raw, bias_all, alog_all, skip_all, grad))
    )
    _, local_pullback = jax.vjp(slab_local, *late[:7])
    local_grads = local_pullback(late[7])
    entering, leaving, local_grads = carry_across(total, local_state, local_source, local_grads)
    _, carry_pullback = jax.vjp(slab_carry, x, b, c, raw, bias_all, alog_all, entering)
    carry_grads = carry_pullback((grad, leaving))[:6]
    gx, gb, gc, graw, gbias, galog = [u + v for u, v in zip(local_grads[:6], carry_grads)]
    gskip = local_grads[6]
    grad_inputs = gx.reshape(tokens, num_heads * P_SIZE).astype(jnp.bfloat16)[None]
    grad_b = gb.reshape(tokens, G * N).astype(jnp.bfloat16)[None]
    grad_c = gc.reshape(tokens, G * N).astype(jnp.bfloat16)[None]
    grad_dt = graw[None]
    head_stats = jnp.stack([galog, gbias, gskip], axis=0)
    count = lax.axis_size("dp")
    share_size = num_heads // count
    dealt = head_stats.reshape(3, count, share_size).transpose(1, 0, 2)
    own_totals = jnp.sum(lax.all_to_all(dealt, "dp", 0, 0, tiled=True), axis=0)
    own_totals = sum_by_butterfly(own_totals, ("ctx",))
    return (grad_inputs, grad_b, grad_c, grad_dt, own_totals[0], own_totals[1], own_totals[2])


def solution(mesh):
    in_specs = (
        P("dp", "ctx", None),
        P("dp", "ctx", None),
        P("dp", "ctx", None),
        P("dp", None, "ctx"),
        P("dp"),
        P("dp"),
        P("dp"),
        P("dp", "ctx", None),
    )
    out_specs = (
        P("dp", "ctx", None),
        P("dp", "ctx", None),
        P("dp", "ctx", None),
        P("dp", None, "ctx"),
        P("dp"),
        P("dp"),
        P("dp"),
    )
    return jax.shard_map(
        per_device, mesh=mesh, in_specs=in_specs, out_specs=out_specs, check_vma=False
    )
```

```python
import jax
import jax.numpy as jnp
from jax import lax
from jax.sharding import PartitionSpec as P

P_SIZE = 64
N = 64
G = 8


highest = lax.Precision.HIGHEST
fast = lax.Precision.HIGH


def slab_prelude(x, raw, bias, alog):
    tokens, num_heads, width = x.shape
    dt_value = jax.nn.softplus(raw + bias[:, None])
    log_decay = dt_value * (-jnp.exp(alog))[:, None]
    cumulative = jnp.cumsum(log_decay, axis=1)
    scaled = (x * dt_value.T[:, :, None]).reshape(tokens, G, num_heads // G, width)
    return cumulative, scaled


def slab_local(x, b, c, raw, bias, alog, skip):
    tokens, num_heads, width = x.shape
    group_heads = num_heads // G
    cumulative, scaled = slab_prelude(x, raw, bias, alog)
    scores = jnp.einsum("qgn,kgn->gqk", c, b, precision=fast)
    offsets = jnp.arange(tokens)
    causal = offsets[:, None] >= offsets[None, :]
    spread = cumulative[:, :, None] - cumulative[:, None, :]
    weights = jnp.where(causal, jnp.exp(jnp.where(causal, spread, 0.0)), 0.0)
    mixed = weights.reshape(G, group_heads, tokens, tokens) * scores[:, None]
    local_part = jnp.einsum("gjqk,kgjp->qgjp", mixed, scaled, precision=fast)
    return local_part.reshape(tokens, num_heads, width) + skip[None, :, None] * x


def slab_carry(x, b, c, raw, bias, alog, state_in):
    tokens, num_heads, width = x.shape
    group_heads = num_heads // G
    cumulative, scaled = slab_prelude(x, raw, bias, alog)
    tail_decay = jnp.exp(cumulative[:, -1:] - cumulative)
    weighted_b = b[:, :, None, :] * tail_decay.T.reshape(tokens, G, group_heads)[:, :, :, None]
    block_state = jnp.einsum("kgjn,kgjp->gjpn", weighted_b, scaled, precision=fast)
    block_state = block_state.reshape(num_heads, width, N)
    state_out = jnp.exp(cumulative[:, -1])[:, None, None] * state_in + block_state
    entering = state_in.reshape(G, group_heads, width, N)
    cross_part = jnp.einsum("qgn,gjpn->qgjp", c, entering, precision=fast)
    cross_part = cross_part * jnp.exp(cumulative).T.reshape(tokens, G, group_heads)[:, :, :, None]
    return (cross_part.reshape(tokens, num_heads, width), state_out)


def slab_terms(x, b, c, raw, bias, alog, grad):
    tokens, num_heads, width = x.shape
    group_heads = num_heads // G
    dt_value = jax.nn.softplus(raw + bias[:, None])
    log_decay = dt_value * (-jnp.exp(alog))[:, None]
    cumulative = jnp.cumsum(log_decay, axis=1)
    total = cumulative[:, -1]
    tail_decay = jnp.exp(total[:, None] - cumulative)
    carried = (x * (dt_value * tail_decay).T[:, :, None]).reshape(tokens, G, group_heads, width)
    local_state = jnp.einsum("tgn,tgjp->gjpn", b, carried, precision=fast)
    weighted_grad = (grad * jnp.exp(cumulative).T[:, :, None]).reshape(tokens, G, group_heads, width)
    local_source = jnp.einsum("tgn,tgjp->gjpn", c, weighted_grad, precision=fast)
    return (
        total,
        local_state.reshape(num_heads, width, N),
        local_source.reshape(num_heads, width, N),
    )


def carry_across(total, local_state, local_source, held):
    count = lax.axis_size("ctx")
    num_heads, width, lanes = local_state.shape
    share = num_heads // count
    rows = width * lanes // 128
    block = share * rows
    states = local_state.reshape(count, block, 128)
    sources = local_source.reshape(count, block, 128)
    totals = jnp.broadcast_to(total.reshape(count, share, 1), (count, share, 128))
    padding = -share % 8
    if padding:
        totals = jnp.concatenate([totals, jnp.zeros((count, padding, 128), totals.dtype)], axis=1)
    payload = jnp.concatenate([states, sources, totals], axis=1)
    chunk = payload.shape[1]
    got = lax.all_to_all(payload.reshape(count * chunk, 128), "ctx", 0, 0, tiled=True)
    got, held = lax.optimization_barrier((got, held))
    got = got.reshape(count, chunk, 128)
    states = got[:, :block].reshape(count * share, rows, 128)
    sources = got[:, block : 2 * block].reshape(count * share, rows, 128)
    totals = got[:, 2 * block : 2 * block + share, 0]
    slab = jnp.arange(count)
    between = (slab[None, :, None] < slab[None, None, :]) & (slab[None, None, :] < slab[:, None, None])
    exponent = jnp.einsum("jim,mh->jih", between.astype(jnp.float32), totals, precision=highest)
    before = slab[None, :] < slab[:, None]
    chain = jnp.where(before[:, :, None], jnp.exp(jnp.where(before[:, :, None], exponent, 0.0)), 0.0)
    same = jnp.eye(share, dtype=chain.dtype)
    spread = (chain[:, :, :, None] * same[None, None]).transpose(0, 2, 1, 3)
    spread = spread.reshape(count * share, count * share)
    entering = jnp.einsum("ab,brl->arl", spread, states, precision=highest)
    leaving = jnp.einsum("ba,brl->arl", spread, sources, precision=highest)
    back = jnp.concatenate(
        [entering.reshape(count, block, 128), leaving.reshape(count, block, 128)], axis=1
    )
    mine = lax.all_to_all(back.reshape(count * 2 * block, 128), "ctx", 0, 0, tiled=True)
    mine = mine.reshape(count, 2 * block, 128)
    entering = mine[:, :block].reshape(num_heads, width, lanes)
    leaving = mine[:, block:].reshape(num_heads, width, lanes)
    return entering, leaving, held


def exchange(value, axis, distance):
    count = lax.axis_size(axis)
    return lax.ppermute(value, axis, [(i, i ^ distance) for i in range(count)])


def group_values(value, axis, stride):
    place = (lax.axis_index(axis) // stride) % 4
    held = [value] + [exchange(value, axis, step * stride) for step in (1, 2, 3)]
    ordered = []
    for position in range(4):
        pick = held[3]
        for step in (2, 1, 0):
            pick = jnp.where((place ^ step) == position, held[step], pick)
        ordered.append(pick)
    return ordered


def gather_by_doubling(value, axis):
    stride = 1
    while stride < lax.axis_size(axis):
        value = jnp.concatenate(group_values(value, axis, stride), axis=-1)
        stride *= 4
    return value


def sum_by_butterfly(value, axes):
    for axis in axes:
        stride = 1
        while stride < lax.axis_size(axis):
            first, second, third, fourth = group_values(value, axis, stride)
            value = (first + second) + (third + fourth)
            stride *= 4
    return value


def per_device(inputs, b_proj, c_proj, dt_raw, a_log, dt_bias, d_skip, grad_out):
    params = gather_by_doubling(jnp.stack([a_log, dt_bias, d_skip]), "dp")
    alog_all, bias_all, skip_all = params[0], params[1], params[2]
    tokens = inputs.shape[1]
    num_heads = alog_all.shape[0]
    x = inputs[0].astype(jnp.float32).reshape(tokens, num_heads, P_SIZE)
    grad = grad_out[0].astype(jnp.float32).reshape(tokens, num_heads, P_SIZE)
    b = b_proj[0].astype(jnp.float32).reshape(tokens, G, N)
    c = c_proj[0].astype(jnp.float32).reshape(tokens, G, N)
    raw = dt_raw[0]
    total, local_state, local_source = slab_terms(x, b, c, raw, bias_all, alog_all, grad)
    (total, local_state, local_source), late = lax.optimization_barrier(
        ((total, local_state, local_source), (x, b, c, raw, bias_all, alog_all, skip_all, grad))
    )
    _, local_pullback = jax.vjp(slab_local, *late[:7])
    local_grads = local_pullback(late[7])
    entering, leaving, local_grads = carry_across(total, local_state, local_source, local_grads)
    _, carry_pullback = jax.vjp(slab_carry, x, b, c, raw, bias_all, alog_all, entering)
    carry_grads = carry_pullback((grad, leaving))[:6]
    gx, gb, gc, graw, gbias, galog = [u + v for u, v in zip(local_grads[:6], carry_grads)]
    gskip = local_grads[6]
    grad_inputs = gx.reshape(tokens, num_heads * P_SIZE).astype(jnp.bfloat16)[None]
    grad_b = gb.reshape(tokens, G * N).astype(jnp.bfloat16)[None]
    grad_c = gc.reshape(tokens, G * N).astype(jnp.bfloat16)[None]
    grad_dt = graw[None]
    head_stats = jnp.stack([galog, gbias, gskip], axis=0)
    count = lax.axis_size("dp")
    share_size = num_heads // count
    dealt = head_stats.reshape(3, count, share_size).transpose(1, 0, 2)
    own_totals = jnp.sum(lax.all_to_all(dealt, "dp", 0, 0, tiled=True), axis=0)
    own_totals = sum_by_butterfly(own_totals, ("ctx",))
    return (grad_inputs, grad_b, grad_c, grad_dt, own_totals[0], own_totals[1], own_totals[2])


def solution(mesh):
    in_specs = (
        P("dp", "ctx", None),
        P("dp", "ctx", None),
        P("dp", "ctx", None),
        P("dp", None, "ctx"),
        P("dp"),
        P("dp"),
        P("dp"),
        P("dp", "ctx", None),
    )
    out_specs = (
        P("dp", "ctx", None),
        P("dp", "ctx", None),
        P("dp", "ctx", None),
        P("dp", None, "ctx"),
        P("dp"),
        P("dp"),
        P("dp"),
    )
    return jax.shard_map(
        per_device, mesh=mesh, in_specs=in_specs, out_specs=out_specs, check_vma=False
    )
```

```python
import jax
import jax.numpy as jnp
from jax import lax
from jax.sharding import PartitionSpec as P

P_SIZE = 64
N = 64
G = 8


highest = lax.Precision.HIGHEST
fast = lax.Precision.HIGH


def slab_prelude(x, raw, bias, alog):
    tokens, num_heads, width = x.shape
    dt_value = jax.nn.softplus(raw + bias[:, None])
    log_decay = dt_value * (-jnp.exp(alog))[:, None]
    cumulative = jnp.cumsum(log_decay, axis=1)
    scaled = (x * dt_value.T[:, :, None]).reshape(tokens, G, num_heads // G, width)
    return cumulative, scaled


def slab_local(x, b, c, raw, bias, alog, skip):
    tokens, num_heads, width = x.shape
    group_heads = num_heads // G
    cumulative, scaled = slab_prelude(x, raw, bias, alog)
    scores = jnp.einsum("qgn,kgn->gqk", c, b, precision=fast)
    offsets = jnp.arange(tokens)
    causal = offsets[:, None] >= offsets[None, :]
    spread = cumulative[:, :, None] - cumulative[:, None, :]
    weights = jnp.where(causal, jnp.exp(jnp.where(causal, spread, 0.0)), 0.0)
    mixed = weights.reshape(G, group_heads, tokens, tokens) * scores[:, None]
    local_part = jnp.einsum("gjqk,kgjp->qgjp", mixed, scaled, precision=fast)
    return local_part.reshape(tokens, num_heads, width) + skip[None, :, None] * x


def slab_carry(x, b, c, raw, bias, alog, state_in):
    tokens, num_heads, width = x.shape
    group_heads = num_heads // G
    cumulative, scaled = slab_prelude(x, raw, bias, alog)
    tail_decay = jnp.exp(cumulative[:, -1:] - cumulative)
    weighted_b = b[:, :, None, :] * tail_decay.T.reshape(tokens, G, group_heads)[:, :, :, None]
    block_state = jnp.einsum("kgjn,kgjp->gjpn", weighted_b, scaled, precision=fast)
    block_state = block_state.reshape(num_heads, width, N)
    state_out = jnp.exp(cumulative[:, -1])[:, None, None] * state_in + block_state
    entering = state_in.reshape(G, group_heads, width, N)
    cross_part = jnp.einsum("qgn,gjpn->qgjp", c, entering, precision=fast)
    cross_part = cross_part * jnp.exp(cumulative).T.reshape(tokens, G, group_heads)[:, :, :, None]
    return (cross_part.reshape(tokens, num_heads, width), state_out)


def slab_terms(x, b, c, raw, bias, alog, grad):
    tokens, num_heads, width = x.shape
    group_heads = num_heads // G
    dt_value = jax.nn.softplus(raw + bias[:, None])
    log_decay = dt_value * (-jnp.exp(alog))[:, None]
    cumulative = jnp.cumsum(log_decay, axis=1)
    total = cumulative[:, -1]
    tail_decay = jnp.exp(total[:, None] - cumulative)
    carried = (x * (dt_value * tail_decay).T[:, :, None]).reshape(tokens, G, group_heads, width)
    weighted_grad = (grad * jnp.exp(cumulative).T[:, :, None]).reshape(tokens, G, group_heads, width)
    both = jnp.einsum(
        "tgwn,tgwjp->wgjpn",
        jnp.stack([b, c], axis=2),
        jnp.stack([carried, weighted_grad], axis=2),
        precision=fast,
    )
    return (total, both.reshape(2, num_heads, width, N))


def carry_across(total, both, held):
    count = lax.axis_size("ctx")
    _, num_heads, width, lanes = both.shape
    share = num_heads // count
    rows = width * lanes // 128
    block = share * rows
    pairs = both.reshape(2, count, block, 128).transpose(1, 0, 2, 3).reshape(count, 2 * block, 128)
    totals = jnp.broadcast_to(total.reshape(count, share, 1), (count, share, 128))
    padding = -share % 8
    if padding:
        totals = jnp.concatenate([totals, jnp.zeros((count, padding, 128), totals.dtype)], axis=1)
    payload = jnp.concatenate([pairs, totals], axis=1)
    chunk = payload.shape[1]
    got = lax.all_to_all(payload.reshape(count * chunk, 128), "ctx", 0, 0, tiled=True)
    got, held = lax.optimization_barrier((got, held))
    got = got.reshape(count, chunk, 128)
    states = got[:, :block].reshape(count * share, rows, 128)
    sources = got[:, block : 2 * block].reshape(count * share, rows, 128)
    totals = got[:, 2 * block : 2 * block + share, 0]
    slab = jnp.arange(count)
    between = (slab[None, :, None] < slab[None, None, :]) & (slab[None, None, :] < slab[:, None, None])
    exponent = jnp.einsum("jim,mh->jih", between.astype(jnp.float32), totals, precision=highest)
    before = slab[None, :] < slab[:, None]
    chain = jnp.where(before[:, :, None], jnp.exp(jnp.where(before[:, :, None], exponent, 0.0)), 0.0)
    same = jnp.eye(share, dtype=chain.dtype)
    spread = (chain[:, :, :, None] * same[None, None]).transpose(0, 2, 1, 3)
    spread = spread.reshape(count * share, count * share)
    entering = jnp.einsum("ab,brl->arl", spread, states, precision=fast)
    leaving = jnp.einsum("ba,brl->arl", spread, sources, precision=fast)
    back = jnp.concatenate(
        [entering.reshape(count, block, 128), leaving.reshape(count, block, 128)], axis=1
    )
    mine = lax.all_to_all(back.reshape(count * 2 * block, 128), "ctx", 0, 0, tiled=True)
    mine = mine.reshape(count, 2 * block, 128)
    entering = mine[:, :block].reshape(num_heads, width, lanes)
    leaving = mine[:, block:].reshape(num_heads, width, lanes)
    return entering, leaving, held


def exchange(value, axis, distance):
    count = lax.axis_size(axis)
    return lax.ppermute(value, axis, [(i, i ^ distance) for i in range(count)])


def group_values(value, axis, stride):
    place = (lax.axis_index(axis) // stride) % 4
    held = [value] + [exchange(value, axis, step * stride) for step in (1, 2, 3)]
    ordered = []
    for position in range(4):
        pick = held[3]
        for step in (2, 1, 0):
            pick = jnp.where((place ^ step) == position, held[step], pick)
        ordered.append(pick)
    return ordered


def gather_by_doubling(value, axis):
    stride = 1
    while stride < lax.axis_size(axis):
        value = jnp.concatenate(group_values(value, axis, stride), axis=-1)
        stride *= 4
    return value


def sum_by_butterfly(value, axes):
    for axis in axes:
        stride = 1
        while stride < lax.axis_size(axis):
            first, second, third, fourth = group_values(value, axis, stride)
            value = (first + second) + (third + fourth)
            stride *= 4
    return value


def per_device(inputs, b_proj, c_proj, dt_raw, a_log, dt_bias, d_skip, grad_out):
    params = gather_by_doubling(jnp.stack([a_log, dt_bias, d_skip]), "dp")
    alog_all, bias_all, skip_all = params[0], params[1], params[2]
    tokens = inputs.shape[1]
    num_heads = alog_all.shape[0]
    x = inputs[0].astype(jnp.float32).reshape(tokens, num_heads, P_SIZE)
    grad = grad_out[0].astype(jnp.float32).reshape(tokens, num_heads, P_SIZE)
    b = b_proj[0].astype(jnp.float32).reshape(tokens, G, N)
    c = c_proj[0].astype(jnp.float32).reshape(tokens, G, N)
    raw = dt_raw[0]
    total, both = slab_terms(x, b, c, raw, bias_all, alog_all, grad)
    (total, both), late = lax.optimization_barrier(
        ((total, both), (x, b, c, raw, bias_all, alog_all, skip_all, grad))
    )
    _, local_pullback = jax.vjp(slab_local, *late[:7])
    local_grads = local_pullback(late[7])
    entering, leaving, local_grads = carry_across(total, both, local_grads)
    _, carry_pullback = jax.vjp(slab_carry, x, b, c, raw, bias_all, alog_all, entering)
    carry_grads = carry_pullback((grad, leaving))[:6]
    gx, gb, gc, graw, gbias, galog = [u + v for u, v in zip(local_grads[:6], carry_grads)]
    gskip = local_grads[6]
    grad_inputs = gx.reshape(tokens, num_heads * P_SIZE).astype(jnp.bfloat16)[None]
    grad_b = gb.reshape(tokens, G * N).astype(jnp.bfloat16)[None]
    grad_c = gc.reshape(tokens, G * N).astype(jnp.bfloat16)[None]
    grad_dt = graw[None]
    head_stats = jnp.stack([galog, gbias, gskip], axis=0)
    count = lax.axis_size("dp")
    share_size = num_heads // count
    dealt = head_stats.reshape(3, count, share_size).transpose(1, 0, 2)
    own_totals = jnp.sum(lax.all_to_all(dealt, "dp", 0, 0, tiled=True), axis=0)
    own_totals = sum_by_butterfly(own_totals, ("ctx",))
    return (grad_inputs, grad_b, grad_c, grad_dt, own_totals[0], own_totals[1], own_totals[2])


def solution(mesh):
    in_specs = (
        P("dp", "ctx", None),
        P("dp", "ctx", None),
        P("dp", "ctx", None),
        P("dp", None, "ctx"),
        P("dp"),
        P("dp"),
        P("dp"),
        P("dp", "ctx", None),
    )
    out_specs = (
        P("dp", "ctx", None),
        P("dp", "ctx", None),
        P("dp", "ctx", None),
        P("dp", None, "ctx"),
        P("dp"),
        P("dp"),
        P("dp"),
    )
    return jax.shard_map(
        per_device, mesh=mesh, in_specs=in_specs, out_specs=out_specs, check_vma=False
    )
```

```python
import jax
import jax.numpy as jnp
from jax import lax
from jax.sharding import PartitionSpec as P

P_SIZE = 64
N = 64
G = 8


highest = lax.Precision.HIGHEST
fast = lax.Precision.HIGH


def running_sum(values):
    tokens = values.shape[-1]
    offsets = jnp.arange(tokens)
    upper = (offsets[:, None] <= offsets[None, :]).astype(values.dtype)
    return jnp.einsum("ht,ts->hs", values, upper, precision=highest)


def slab_prelude(x, raw, bias, alog):
    tokens, num_heads, width = x.shape
    dt_value = jax.nn.softplus(raw + bias[:, None])
    log_decay = dt_value * (-jnp.exp(alog))[:, None]
    cumulative = running_sum(log_decay)
    scaled = (x * dt_value.T[:, :, None]).reshape(tokens, G, num_heads // G, width)
    return cumulative, scaled


def slab_local(x, b, c, raw, bias, alog, skip):
    tokens, num_heads, width = x.shape
    group_heads = num_heads // G
    cumulative, scaled = slab_prelude(x, raw, bias, alog)
    scores = jnp.einsum("qgn,kgn->gqk", c, b, precision=fast)
    offsets = jnp.arange(tokens)
    causal = offsets[:, None] >= offsets[None, :]
    spread = cumulative[:, :, None] - cumulative[:, None, :]
    weights = jnp.where(causal, jnp.exp(jnp.where(causal, spread, 0.0)), 0.0)
    mixed = weights.reshape(G, group_heads, tokens, tokens) * scores[:, None]
    local_part = jnp.einsum("gjqk,kgjp->qgjp", mixed, scaled, precision=fast)
    return local_part.reshape(tokens, num_heads, width) + skip[None, :, None] * x


def slab_carry(x, b, c, raw, bias, alog, state_in):
    tokens, num_heads, width = x.shape
    group_heads = num_heads // G
    cumulative, scaled = slab_prelude(x, raw, bias, alog)
    tail_decay = jnp.exp(cumulative[:, -1:] - cumulative)
    weighted_b = b[:, :, None, :] * tail_decay.T.reshape(tokens, G, group_heads)[:, :, :, None]
    block_state = jnp.einsum("kgjn,kgjp->gjpn", weighted_b, scaled, precision=fast)
    block_state = block_state.reshape(num_heads, width, N)
    state_out = jnp.exp(cumulative[:, -1])[:, None, None] * state_in + block_state
    entering = state_in.reshape(G, group_heads, width, N)
    cross_part = jnp.einsum("qgn,gjpn->qgjp", c, entering, precision=fast)
    cross_part = cross_part * jnp.exp(cumulative).T.reshape(tokens, G, group_heads)[:, :, :, None]
    return (cross_part.reshape(tokens, num_heads, width), state_out)


def slab_terms(x, b, c, raw, bias, alog, grad):
    tokens, num_heads, width = x.shape
    group_heads = num_heads // G
    dt_value = jax.nn.softplus(raw + bias[:, None])
    log_decay = dt_value * (-jnp.exp(alog))[:, None]
    cumulative = running_sum(log_decay)
    total = cumulative[:, -1]
    tail_decay = jnp.exp(total[:, None] - cumulative)
    carried = (x * (dt_value * tail_decay).T[:, :, None]).reshape(tokens, G, group_heads, width)
    local_state = jnp.einsum("tgn,tgjp->gjpn", b, carried, precision=fast)
    weighted_grad = (grad * jnp.exp(cumulative).T[:, :, None]).reshape(tokens, G, group_heads, width)
    local_source = jnp.einsum("tgn,tgjp->gjpn", c, weighted_grad, precision=fast)
    return (
        total,
        local_state.reshape(num_heads, width, N),
        local_source.reshape(num_heads, width, N),
    )


def carry_across(total, local_state, local_source, held):
    count = lax.axis_size("ctx")
    num_heads, width, lanes = local_state.shape
    share = num_heads // count
    rows = width * lanes // 128
    block = share * rows
    states = local_state.reshape(count, block, 128)
    sources = local_source.reshape(count, block, 128)
    totals = jnp.broadcast_to(total.reshape(count, share, 1), (count, share, 128))
    padding = -share % 8
    if padding:
        totals = jnp.concatenate([totals, jnp.zeros((count, padding, 128), totals.dtype)], axis=1)
    payload = jnp.concatenate([states, sources, totals], axis=1)
    chunk = payload.shape[1]
    got = lax.all_to_all(payload.reshape(count * chunk, 128), "ctx", 0, 0, tiled=True)
    got, held = lax.optimization_barrier((got, held))
    got = got.reshape(count, chunk, 128)
    states = got[:, :block].reshape(count * share, rows, 128)
    sources = got[:, block : 2 * block].reshape(count * share, rows, 128)
    totals = got[:, 2 * block : 2 * block + share, 0]
    slab = jnp.arange(count)
    between = (slab[None, :, None] < slab[None, None, :]) & (slab[None, None, :] < slab[:, None, None])
    exponent = jnp.einsum("jim,mh->jih", between.astype(jnp.float32), totals, precision=highest)
    before = slab[None, :] < slab[:, None]
    chain = jnp.where(before[:, :, None], jnp.exp(jnp.where(before[:, :, None], exponent, 0.0)), 0.0)
    same = jnp.eye(share, dtype=chain.dtype)
    spread = (chain[:, :, :, None] * same[None, None]).transpose(0, 2, 1, 3)
    spread = spread.reshape(count * share, count * share)
    entering = jnp.einsum("ab,brl->arl", spread, states, precision=highest)
    leaving = jnp.einsum("ba,brl->arl", spread, sources, precision=highest)
    back = jnp.concatenate(
        [entering.reshape(count, block, 128), leaving.reshape(count, block, 128)], axis=1
    )
    mine = lax.all_to_all(back.reshape(count * 2 * block, 128), "ctx", 0, 0, tiled=True)
    mine = mine.reshape(count, 2 * block, 128)
    entering = mine[:, :block].reshape(num_heads, width, lanes)
    leaving = mine[:, block:].reshape(num_heads, width, lanes)
    return entering, leaving, held


def exchange(value, axis, distance):
    count = lax.axis_size(axis)
    return lax.ppermute(value, axis, [(i, i ^ distance) for i in range(count)])


def group_values(value, axis, stride):
    place = (lax.axis_index(axis) // stride) % 4
    held = [value] + [exchange(value, axis, step * stride) for step in (1, 2, 3)]
    ordered = []
    for position in range(4):
        pick = held[3]
        for step in (2, 1, 0):
            pick = jnp.where((place ^ step) == position, held[step], pick)
        ordered.append(pick)
    return ordered


def gather_by_doubling(value, axis):
    stride = 1
    while stride < lax.axis_size(axis):
        value = jnp.concatenate(group_values(value, axis, stride), axis=-1)
        stride *= 4
    return value


def sum_by_butterfly(value, axes):
    for axis in axes:
        stride = 1
        while stride < lax.axis_size(axis):
            first, second, third, fourth = group_values(value, axis, stride)
            value = (first + second) + (third + fourth)
            stride *= 4
    return value


def per_device(inputs, b_proj, c_proj, dt_raw, a_log, dt_bias, d_skip, grad_out):
    params = gather_by_doubling(jnp.stack([a_log, dt_bias, d_skip]), "dp")
    alog_all, bias_all, skip_all = params[0], params[1], params[2]
    tokens = inputs.shape[1]
    num_heads = alog_all.shape[0]
    x = inputs[0].astype(jnp.float32).reshape(tokens, num_heads, P_SIZE)
    grad = grad_out[0].astype(jnp.float32).reshape(tokens, num_heads, P_SIZE)
    b = b_proj[0].astype(jnp.float32).reshape(tokens, G, N)
    c = c_proj[0].astype(jnp.float32).reshape(tokens, G, N)
    raw = dt_raw[0]
    total, local_state, local_source = slab_terms(x, b, c, raw, bias_all, alog_all, grad)
    (total, local_state, local_source), late = lax.optimization_barrier(
        ((total, local_state, local_source), (x, b, c, raw, bias_all, alog_all, skip_all, grad))
    )
    _, local_pullback = jax.vjp(slab_local, *late[:7])
    local_grads = local_pullback(late[7])
    entering, leaving, local_grads = carry_across(total, local_state, local_source, local_grads)
    _, carry_pullback = jax.vjp(slab_carry, x, b, c, raw, bias_all, alog_all, entering)
    carry_grads = carry_pullback((grad, leaving))[:6]
    gx, gb, gc, graw, gbias, galog = [u + v for u, v in zip(local_grads[:6], carry_grads)]
    gskip = local_grads[6]
    grad_inputs = gx.reshape(tokens, num_heads * P_SIZE).astype(jnp.bfloat16)[None]
    grad_b = gb.reshape(tokens, G * N).astype(jnp.bfloat16)[None]
    grad_c = gc.reshape(tokens, G * N).astype(jnp.bfloat16)[None]
    grad_dt = graw[None]
    head_stats = jnp.stack([galog, gbias, gskip], axis=0)
    count = lax.axis_size("dp")
    share_size = num_heads // count
    dealt = head_stats.reshape(3, count, share_size).transpose(1, 0, 2)
    own_totals = jnp.sum(lax.all_to_all(dealt, "dp", 0, 0, tiled=True), axis=0)
    own_totals = sum_by_butterfly(own_totals, ("ctx",))
    return (grad_inputs, grad_b, grad_c, grad_dt, own_totals[0], own_totals[1], own_totals[2])


def solution(mesh):
    in_specs = (
        P("dp", "ctx", None),
        P("dp", "ctx", None),
        P("dp", "ctx", None),
        P("dp", None, "ctx"),
        P("dp"),
        P("dp"),
        P("dp"),
        P("dp", "ctx", None),
    )
    out_specs = (
        P("dp", "ctx", None),
        P("dp", "ctx", None),
        P("dp", "ctx", None),
        P("dp", None, "ctx"),
        P("dp"),
        P("dp"),
        P("dp"),
    )
    return jax.shard_map(
        per_device, mesh=mesh, in_specs=in_specs, out_specs=out_specs, check_vma=False
    )
```

```python
import jax
import jax.numpy as jnp
from jax import lax
from jax.sharding import PartitionSpec as P

P_SIZE = 64
N = 64
G = 8


highest = lax.Precision.HIGHEST
fast = lax.Precision.HIGH


def running_sum(values):
    tokens = values.shape[-1]
    offsets = jnp.arange(tokens)
    upper = (offsets[:, None] <= offsets[None, :]).astype(values.dtype)
    return jnp.einsum("ht,ts->hs", values, upper, precision=highest)


def slab_prelude(x, raw, bias, alog):
    tokens, num_heads, width = x.shape
    dt_value = jax.nn.softplus(raw + bias[:, None])
    log_decay = dt_value * (-jnp.exp(alog))[:, None]
    cumulative = running_sum(log_decay)
    scaled = (x * dt_value.T[:, :, None]).reshape(tokens, G, num_heads // G, width)
    return cumulative, scaled


def slab_local(x, b, c, raw, bias, alog, skip):
    tokens, num_heads, width = x.shape
    group_heads = num_heads // G
    cumulative, scaled = slab_prelude(x, raw, bias, alog)
    scores = jnp.einsum("qgn,kgn->gqk", c, b, precision=fast)
    offsets = jnp.arange(tokens)
    causal = offsets[:, None] >= offsets[None, :]
    spread = cumulative[:, :, None] - cumulative[:, None, :]
    weights = jnp.where(causal, jnp.exp(jnp.where(causal, spread, 0.0)), 0.0)
    mixed = weights.reshape(G, group_heads, tokens, tokens) * scores[:, None]
    local_part = jnp.einsum("gjqk,kgjp->qgjp", mixed, scaled, precision=fast)
    return local_part.reshape(tokens, num_heads, width) + skip[None, :, None] * x


def slab_carry(x, b, c, raw, bias, alog, state_in):
    tokens, num_heads, width = x.shape
    group_heads = num_heads // G
    cumulative, scaled = slab_prelude(x, raw, bias, alog)
    tail_decay = jnp.exp(cumulative[:, -1:] - cumulative)
    weighted_b = b[:, :, None, :] * tail_decay.T.reshape(tokens, G, group_heads)[:, :, :, None]
    block_state = jnp.einsum("kgjn,kgjp->gjpn", weighted_b, scaled, precision=fast)
    block_state = block_state.reshape(num_heads, width, N)
    state_out = jnp.exp(cumulative[:, -1])[:, None, None] * state_in + block_state
    entering = state_in.reshape(G, group_heads, width, N)
    cross_part = jnp.einsum("qgn,gjpn->qgjp", c, entering, precision=fast)
    cross_part = cross_part * jnp.exp(cumulative).T.reshape(tokens, G, group_heads)[:, :, :, None]
    return (cross_part.reshape(tokens, num_heads, width), state_out)


def slab_terms(x, b, c, raw, bias, alog, grad):
    tokens, num_heads, width = x.shape
    group_heads = num_heads // G
    dt_value = jax.nn.softplus(raw + bias[:, None])
    log_decay = dt_value * (-jnp.exp(alog))[:, None]
    cumulative = running_sum(log_decay)
    total = cumulative[:, -1]
    tail_decay = jnp.exp(total[:, None] - cumulative)
    carried = (x * (dt_value * tail_decay).T[:, :, None]).reshape(tokens, G, group_heads, width)
    local_state = jnp.einsum("tgn,tgjp->gjpn", b, carried, precision=fast)
    weighted_grad = (grad * jnp.exp(cumulative).T[:, :, None]).reshape(tokens, G, group_heads, width)
    local_source = jnp.einsum("tgn,tgjp->gjpn", c, weighted_grad, precision=fast)
    return (
        total,
        local_state.reshape(num_heads, width, N),
        local_source.reshape(num_heads, width, N),
    )


def carry_across(total, local_state, local_source, held):
    count = lax.axis_size("ctx")
    num_heads, width, lanes = local_state.shape
    share = num_heads // count
    rows = width * lanes // 128
    block = share * rows
    states = local_state.reshape(count, block, 128)
    sources = local_source.reshape(count, block, 128)
    totals = jnp.broadcast_to(total.reshape(count, share, 1), (count, share, 128))
    padding = -share % 8
    if padding:
        totals = jnp.concatenate([totals, jnp.zeros((count, padding, 128), totals.dtype)], axis=1)
    payload = jnp.concatenate([states, sources, totals], axis=1)
    chunk = payload.shape[1]
    got = lax.all_to_all(payload.reshape(count * chunk, 128), "ctx", 0, 0, tiled=True)
    got, held = lax.optimization_barrier((got, held))
    got = got.reshape(count, chunk, 128)
    states = got[:, :block].reshape(count * share, rows, 128)
    sources = got[:, block : 2 * block].reshape(count * share, rows, 128)
    totals = got[:, 2 * block : 2 * block + share, 0]
    slab = jnp.arange(count)
    between = (slab[None, :, None] < slab[None, None, :]) & (slab[None, None, :] < slab[:, None, None])
    exponent = jnp.einsum("jim,mh->jih", between.astype(jnp.float32), totals, precision=highest)
    before = slab[None, :] < slab[:, None]
    chain = jnp.where(before[:, :, None], jnp.exp(jnp.where(before[:, :, None], exponent, 0.0)), 0.0)
    same = jnp.eye(share, dtype=chain.dtype)
    spread = (chain[:, :, :, None] * same[None, None]).transpose(0, 2, 1, 3)
    spread = spread.reshape(count * share, count * share)
    entering = jnp.einsum("ab,brl->arl", spread, states, precision=fast)
    leaving = jnp.einsum("ba,brl->arl", spread, sources, precision=fast)
    back = jnp.concatenate(
        [entering.reshape(count, block, 128), leaving.reshape(count, block, 128)], axis=1
    )
    mine = lax.all_to_all(back.reshape(count * 2 * block, 128), "ctx", 0, 0, tiled=True)
    mine = mine.reshape(count, 2 * block, 128)
    entering = mine[:, :block].reshape(num_heads, width, lanes)
    leaving = mine[:, block:].reshape(num_heads, width, lanes)
    return entering, leaving, held


def exchange(value, axis, distance):
    count = lax.axis_size(axis)
    return lax.ppermute(value, axis, [(i, i ^ distance) for i in range(count)])


def group_values(value, axis, stride):
    place = (lax.axis_index(axis) // stride) % 4
    held = [value] + [exchange(value, axis, step * stride) for step in (1, 2, 3)]
    ordered = []
    for position in range(4):
        pick = held[3]
        for step in (2, 1, 0):
            pick = jnp.where((place ^ step) == position, held[step], pick)
        ordered.append(pick)
    return ordered


def gather_by_doubling(value, axis):
    stride = 1
    while stride < lax.axis_size(axis):
        value = jnp.concatenate(group_values(value, axis, stride), axis=-1)
        stride *= 4
    return value


def sum_by_butterfly(value, axes):
    for axis in axes:
        stride = 1
        while stride < lax.axis_size(axis):
            first, second, third, fourth = group_values(value, axis, stride)
            value = (first + second) + (third + fourth)
            stride *= 4
    return value


def per_device(inputs, b_proj, c_proj, dt_raw, a_log, dt_bias, d_skip, grad_out):
    params = gather_by_doubling(jnp.stack([a_log, dt_bias, d_skip]), "dp")
    alog_all, bias_all, skip_all = params[0], params[1], params[2]
    tokens = inputs.shape[1]
    num_heads = alog_all.shape[0]
    x = inputs[0].astype(jnp.float32).reshape(tokens, num_heads, P_SIZE)
    grad = grad_out[0].astype(jnp.float32).reshape(tokens, num_heads, P_SIZE)
    b = b_proj[0].astype(jnp.float32).reshape(tokens, G, N)
    c = c_proj[0].astype(jnp.float32).reshape(tokens, G, N)
    raw = dt_raw[0]
    total, local_state, local_source = slab_terms(x, b, c, raw, bias_all, alog_all, grad)
    (total, local_state, local_source), late = lax.optimization_barrier(
        ((total, local_state, local_source), (x, b, c, raw, bias_all, alog_all, skip_all, grad))
    )
    _, local_pullback = jax.vjp(slab_local, *late[:7])
    local_grads = local_pullback(late[7])
    entering, leaving, local_grads = carry_across(total, local_state, local_source, local_grads)
    _, carry_pullback = jax.vjp(slab_carry, x, b, c, raw, bias_all, alog_all, entering)
    carry_grads = carry_pullback((grad, leaving))[:6]
    gx, gb, gc, graw, gbias, galog = [u + v for u, v in zip(local_grads[:6], carry_grads)]
    gskip = local_grads[6]
    grad_inputs = gx.reshape(tokens, num_heads * P_SIZE).astype(jnp.bfloat16)[None]
    grad_b = gb.reshape(tokens, G * N).astype(jnp.bfloat16)[None]
    grad_c = gc.reshape(tokens, G * N).astype(jnp.bfloat16)[None]
    grad_dt = graw[None]
    head_stats = jnp.stack([galog, gbias, gskip], axis=0)
    count = lax.axis_size("dp")
    share_size = num_heads // count
    dealt = head_stats.reshape(3, count, share_size).transpose(1, 0, 2)
    own_totals = jnp.sum(lax.all_to_all(dealt, "dp", 0, 0, tiled=True), axis=0)
    own_totals = sum_by_butterfly(own_totals, ("ctx",))
    return (grad_inputs, grad_b, grad_c, grad_dt, own_totals[0], own_totals[1], own_totals[2])


def solution(mesh):
    in_specs = (
        P("dp", "ctx", None),
        P("dp", "ctx", None),
        P("dp", "ctx", None),
        P("dp", None, "ctx"),
        P("dp"),
        P("dp"),
        P("dp"),
        P("dp", "ctx", None),
    )
    out_specs = (
        P("dp", "ctx", None),
        P("dp", "ctx", None),
        P("dp", "ctx", None),
        P("dp", None, "ctx"),
        P("dp"),
        P("dp"),
        P("dp"),
    )
    return jax.shard_map(
        per_device, mesh=mesh, in_specs=in_specs, out_specs=out_specs, check_vma=False
    )
```

```python
import jax
import jax.numpy as jnp
from jax import lax
from jax.sharding import PartitionSpec as P

P_SIZE = 64
N = 64
G = 8


highest = lax.Precision.HIGHEST
fast = lax.Precision.HIGH


def running_sum(values):
    tokens = values.shape[-1]
    offsets = jnp.arange(tokens)
    upper = (offsets[:, None] <= offsets[None, :]).astype(values.dtype)
    return jnp.einsum("ht,ts->hs", values, upper, precision=highest)


def slab_prelude(x, raw, bias, alog):
    tokens, num_heads, width = x.shape
    dt_value = jax.nn.softplus(raw + bias[:, None])
    log_decay = dt_value * (-jnp.exp(alog))[:, None]
    cumulative = running_sum(log_decay)
    scaled = (x * dt_value.T[:, :, None]).reshape(tokens, G, num_heads // G, width)
    return cumulative, scaled


def slab_local(x, b, c, raw, bias, alog, skip):
    tokens, num_heads, width = x.shape
    group_heads = num_heads // G
    cumulative, scaled = slab_prelude(x, raw, bias, alog)
    scores = jnp.einsum("qgn,kgn->gqk", c, b, precision=fast)
    offsets = jnp.arange(tokens)
    causal = offsets[:, None] >= offsets[None, :]
    spread = cumulative[:, :, None] - cumulative[:, None, :]
    weights = jnp.where(causal, jnp.exp(jnp.where(causal, spread, 0.0)), 0.0)
    mixed = weights.reshape(G, group_heads, tokens, tokens) * scores[:, None]
    local_part = jnp.einsum("gjqk,kgjp->qgjp", mixed, scaled, precision=fast)
    return local_part.reshape(tokens, num_heads, width) + skip[None, :, None] * x


def slab_carry(x, b, c, raw, bias, alog, state_in):
    tokens, num_heads, width = x.shape
    group_heads = num_heads // G
    cumulative, scaled = slab_prelude(x, raw, bias, alog)
    tail_decay = jnp.exp(cumulative[:, -1:] - cumulative)
    weighted_b = b[:, :, None, :] * tail_decay.T.reshape(tokens, G, group_heads)[:, :, :, None]
    block_state = jnp.einsum("kgjn,kgjp->gjpn", weighted_b, scaled, precision=fast)
    block_state = block_state.reshape(num_heads, width, N)
    state_out = jnp.exp(cumulative[:, -1])[:, None, None] * state_in + block_state
    entering = state_in.reshape(G, group_heads, width, N)
    cross_part = jnp.einsum("qgn,gjpn->qgjp", c, entering, precision=fast)
    cross_part = cross_part * jnp.exp(cumulative).T.reshape(tokens, G, group_heads)[:, :, :, None]
    return (cross_part.reshape(tokens, num_heads, width), state_out)


def slab_terms(x, b, c, raw, bias, alog, grad):
    tokens, num_heads, width = x.shape
    group_heads = num_heads // G
    dt_value = jax.nn.softplus(raw + bias[:, None])
    log_decay = dt_value * (-jnp.exp(alog))[:, None]
    cumulative = running_sum(log_decay)
    total = cumulative[:, -1]
    tail_decay = jnp.exp(total[:, None] - cumulative)
    carried = (x * (dt_value * tail_decay).T[:, :, None]).reshape(tokens, G, group_heads, width)
    local_state = jnp.einsum("tgn,tgjp->gjpn", b, carried, precision=fast)
    weighted_grad = (grad * jnp.exp(cumulative).T[:, :, None]).reshape(tokens, G, group_heads, width)
    local_source = jnp.einsum("tgn,tgjp->gjpn", c, weighted_grad, precision=fast)
    return (
        total,
        local_state.reshape(num_heads, width, N),
        local_source.reshape(num_heads, width, N),
    )


def carry_across(total, local_state, local_source, held):
    count = lax.axis_size("ctx")
    num_heads, width, lanes = local_state.shape
    share = num_heads // count
    rows = width * lanes // 128
    block = share * rows
    states = local_state.reshape(count, block, 128)
    sources = local_source.reshape(count, block, 128)
    totals = jnp.broadcast_to(total.reshape(count, share, 1), (count, share, 128))
    padding = -share % 8
    if padding:
        totals = jnp.concatenate([totals, jnp.zeros((count, padding, 128), totals.dtype)], axis=1)
    payload = jnp.concatenate([states, sources, totals], axis=1)
    chunk = payload.shape[1]
    got = lax.all_to_all(payload.reshape(count * chunk, 128), "ctx", 0, 0, tiled=True)
    got, held = lax.optimization_barrier((got, held))
    got = got.reshape(count, chunk, 128)
    states = got[:, :block].reshape(count * share, rows, 128)
    sources = got[:, block : 2 * block].reshape(count * share, rows, 128)
    totals = got[:, 2 * block : 2 * block + share, 0]
    slab = jnp.arange(count)
    between = (slab[None, :, None] < slab[None, None, :]) & (slab[None, None, :] < slab[:, None, None])
    exponent = jnp.einsum("jim,mh->jih", between.astype(jnp.float32), totals, precision=highest)
    before = slab[None, :] < slab[:, None]
    chain = jnp.where(before[:, :, None], jnp.exp(jnp.where(before[:, :, None], exponent, 0.0)), 0.0)
    same = jnp.eye(share, dtype=chain.dtype)
    spread = (chain[:, :, :, None] * same[None, None]).transpose(0, 2, 1, 3)
    spread = spread.reshape(count * share, count * share)
    entering = jnp.einsum("ab,brl->arl", spread, states, precision=fast)
    leaving = jnp.einsum("ba,brl->arl", spread, sources, precision=fast)
    back = jnp.concatenate(
        [entering.reshape(count, block, 128), leaving.reshape(count, block, 128)], axis=1
    )
    mine = lax.all_to_all(back.reshape(count * 2 * block, 128), "ctx", 0, 0, tiled=True)
    mine = mine.reshape(count, 2 * block, 128)
    entering = mine[:, :block].reshape(num_heads, width, lanes)
    leaving = mine[:, block:].reshape(num_heads, width, lanes)
    return entering, leaving, held


def exchange(value, axis, distance):
    count = lax.axis_size(axis)
    return lax.ppermute(value, axis, [(i, i ^ distance) for i in range(count)])


def group_values(value, axis, stride):
    place = (lax.axis_index(axis) // stride) % 4
    held = [value] + [exchange(value, axis, step * stride) for step in (1, 2, 3)]
    ordered = []
    for position in range(4):
        pick = held[3]
        for step in (2, 1, 0):
            pick = jnp.where((place ^ step) == position, held[step], pick)
        ordered.append(pick)
    return ordered


def gather_by_doubling(value, axis):
    stride = 1
    while stride < lax.axis_size(axis):
        value = jnp.concatenate(group_values(value, axis, stride), axis=-1)
        stride *= 4
    return value


def sum_by_butterfly(value, axes):
    for axis in axes:
        stride = 1
        while stride < lax.axis_size(axis):
            first, second, third, fourth = group_values(value, axis, stride)
            value = (first + second) + (third + fourth)
            stride *= 4
    return value


def per_device(inputs, b_proj, c_proj, dt_raw, a_log, dt_bias, d_skip, grad_out):
    params = gather_by_doubling(jnp.stack([a_log, dt_bias, d_skip]), "dp")
    alog_all, bias_all, skip_all = params[0], params[1], params[2]
    tokens = inputs.shape[1]
    num_heads = alog_all.shape[0]
    x = inputs[0].astype(jnp.float32).reshape(tokens, num_heads, P_SIZE)
    grad = grad_out[0].astype(jnp.float32).reshape(tokens, num_heads, P_SIZE)
    b = b_proj[0].astype(jnp.float32).reshape(tokens, G, N)
    c = c_proj[0].astype(jnp.float32).reshape(tokens, G, N)
    raw = dt_raw[0]
    total, local_state, local_source = slab_terms(x, b, c, raw, bias_all, alog_all, grad)
    _, local_pullback = jax.vjp(slab_local, x, b, c, raw, bias_all, alog_all, skip_all)
    local_grads = local_pullback(grad)
    entering, leaving, local_grads = carry_across(total, local_state, local_source, local_grads)
    _, carry_pullback = jax.vjp(slab_carry, x, b, c, raw, bias_all, alog_all, entering)
    carry_grads = carry_pullback((grad, leaving))[:6]
    gx, gb, gc, graw, gbias, galog = [u + v for u, v in zip(local_grads[:6], carry_grads)]
    gskip = local_grads[6]
    grad_inputs = gx.reshape(tokens, num_heads * P_SIZE).astype(jnp.bfloat16)[None]
    grad_b = gb.reshape(tokens, G * N).astype(jnp.bfloat16)[None]
    grad_c = gc.reshape(tokens, G * N).astype(jnp.bfloat16)[None]
    grad_dt = graw[None]
    head_stats = jnp.stack([galog, gbias, gskip], axis=0)
    count = lax.axis_size("dp")
    share_size = num_heads // count
    dealt = head_stats.reshape(3, count, share_size).transpose(1, 0, 2)
    own_totals = jnp.sum(lax.all_to_all(dealt, "dp", 0, 0, tiled=True), axis=0)
    own_totals = sum_by_butterfly(own_totals, ("ctx",))
    return (grad_inputs, grad_b, grad_c, grad_dt, own_totals[0], own_totals[1], own_totals[2])


def solution(mesh):
    in_specs = (
        P("dp", "ctx", None),
        P("dp", "ctx", None),
        P("dp", "ctx", None),
        P("dp", None, "ctx"),
        P("dp"),
        P("dp"),
        P("dp"),
        P("dp", "ctx", None),
    )
    out_specs = (
        P("dp", "ctx", None),
        P("dp", "ctx", None),
        P("dp", "ctx", None),
        P("dp", None, "ctx"),
        P("dp"),
        P("dp"),
        P("dp"),
    )
    return jax.shard_map(
        per_device, mesh=mesh, in_specs=in_specs, out_specs=out_specs, check_vma=False
    )
```
